512 devices in a mesh: tm: 32 (over x_hi, y, core), cell: 16 (over z, x_lo).
Axes of the slice: x: 4 (x_hi: 2, x_lo: 2; x = x_hi * 2 + x_lo), y: 8, z: 8, core: 2. Of those that a mesh axis runs over, the one named last changes fastest.
Arguments:
- start_states: float32 [32, 3, 128, 2048], P('tm', None, None, 'cell'), may hold values from -6 to 6
- ocean_mask: int32 [128, 2048], P(None, 'cell'), may hold values 0 or 1
- depth_class: int32 [128, 2048], P(None, 'cell'), may hold values from 0 to 7
- class_depth: float32 [8], replicated, may hold values from 0.2 to 1
- drag_rate: float32 [128, 2048], P(None, 'cell'), may hold values from 0.02 to 0.3
- tide_cos: float32 [128, 2048], P(None, 'cell'), may hold values from -3 to 3
- tide_sin: float32 [128, 2048], P(None, 'cell'), may hold values from -3 to 3
Outputs:
- defect: float32 [32, 3, 128, 2048], P('tm', None, None, 'cell')
- state_grad: float32 [32, 3, 128, 2048], P('tm', None, None, 'cell')
- drag_grad: float32 [128, 2048], P('tm', 'cell')
The draws below stay inside these ranges and needn't reach their ends.
All inputs are finite; a program needn't handle non-finite values. No bound on the sum of `ocean_mask` on one device may be relied on, other than what follows from the above.
Results may differ from the reference program's by a relative error of at most 0.00002.
Values sent between devices are 32-bit elements; how exact they have to be, the bound alone decides.
No kernel may reach another device: no remote copies, remote signals or barrier semaphores. Data moves between devices by JAX's collectives and lax.ppermute only.
A program may use at most 64 MiB of HBM per device.

```python
import math
import jax
import jax.numpy as jnp
from jax import lax

LAT = 128
STEPS = 8
NCLASS = 8
LON = 2048
SLICES = 32


def touch_ends(entries, own_key, low, largest):
    longest = entries.shape.index(max(entries.shape))
    spots = []
    for shift in (0, 1):
        where = [jax.random.randint(jax.random.fold_in(own_key, axis), (), 0, length) for axis, length in enumerate(entries.shape)]
        where[longest] = (where[longest] + shift) % entries.shape[longest]
        spots.append(tuple(where))
    return entries.at[spots[0]].set(low).at[spots[1]].set(largest)


def strengthened(array, rng, source, target, shards_of, factor):
    owner, partner = [(jnp.arange(array.shape[axis_at]) // (array.shape[axis_at] // shards_of)).reshape([-1 if axis == axis_at else 1 for axis in range(array.ndim)]) for axis_at in (source, target)]
    chosen = jax.random.permutation(rng, shards_of)[partner]
    strong = (owner == chosen) | (owner == (partner + shards_of // 2) % shards_of)
    return jnp.where(strong, factor * array, array)


def block_scale(key, dims, pieces, least, high):
    gain, own = 1.0, jax.random.fold_in(key, 6)
    for dim, parts in pieces:
        draws = jnp.exp(jax.random.uniform(jax.random.fold_in(own, dim), (parts,), jnp.float32, least / len(pieces), high / len(pieces)))
        gain = gain * jnp.repeat(draws, dims[dim] // parts).reshape([-1 if axis == dim else 1 for axis in range(len(dims))])
    return gain


def noise(own_key, extent, scale, most, pieces=(), kind=jnp.bfloat16):
    result = jax.random.normal(own_key, extent, jnp.float32) * scale
    if len(pieces) > 0:
        result = block_scale(own_key, extent, pieces, -0.22, 0.18) * result
    return jnp.clip(result, min=-most, max=most).astype(kind)


def noise_with(key, shape, scale, most, cuts, heavy, kind=jnp.bfloat16):
    result = scale * jax.random.normal(key, shape, jnp.float32)
    if cuts:
        result = result * block_scale(key, shape, cuts, -0.22, 0.18)
    return jnp.clip(strengthened(result, jax.random.fold_in(key, 3), *heavy), -most, most).astype(kind)


def setup_inputs(seed: int = 0) -> dict:
    key_list = jax.random.split(jax.random.key(seed), 8)
    return {
        "start_states": noise_with(key_list[0], (SLICES, 3, LAT, LON), 1.0, 6.0, ((0, 32), (3, 16)), (0, 2, 32, 2.75), jnp.float32),
        "ocean_mask": touch_ends((jax.random.randint(key_list[1], (LAT, LON), 0, 4) < 3).astype(jnp.int32), jax.random.fold_in(key_list[1], 1), 0, 1),
        "depth_class": touch_ends(jax.random.randint(key_list[2], (LAT, LON), 0, NCLASS), jax.random.fold_in(key_list[2], 1), 0, NCLASS - 1).astype(jnp.int32),
        "class_depth": jnp.clip(jax.random.uniform(key_list[3], (NCLASS,), jnp.float32, 0.2, 1.0), 0.2, 1.0),
        "drag_rate": jnp.clip(jnp.exp(math.log(0.3) - 2.7080503 * jax.random.uniform(key_list[4], (LAT, LON), jnp.float32) ** block_scale(key_list[4], (LAT, LON), ((1, 16),), -0.2, 0.2)), 0.02, 0.3),
        "tide_cos": noise(key_list[5], (LAT, LON), 0.5, 3.0, ((1, 16),), jnp.float32),
        "tide_sin": noise(key_list[6], (LAT, LON), 0.5, 3.0, ((1, 16),), jnp.float32),
    }


FLUX_RATE = 0.7
PRESS_RATE = 0.7
ROTATION_RATE = 0.15

def across_cols(values_in):
    return 0.5 * (jnp.roll(values_in, -1, axis=-1) - jnp.roll(values_in, 1, axis=-1))

def across_rows(values_in):
    zeros_row = jnp.zeros_like(values_in[..., :1, :])
    upper_rows = jnp.concatenate([values_in[..., 1:, :], zeros_row], axis=-2)
    lower_rows = jnp.concatenate([zeros_row, values_in[..., :-1, :]], axis=-2)
    return 0.5 * (upper_rows - lower_rows)

def coriolis(rows_count):
    latitude = math.pi * ((jnp.arange(rows_count, dtype=jnp.float32) + 0.5) / rows_count - 0.5)
    return (ROTATION_RATE * jnp.sin(latitude))[:, None]

def advance(current, sea_mask, depth_field, retain, forcing, rotation):
    spread = across_cols(depth_field * current[1]) + across_rows(depth_field * current[2])
    height = sea_mask * (current[0] - FLUX_RATE * spread)
    surface = height + forcing
    mask_keep = sea_mask * retain
    east_new = mask_keep * (current[1] - PRESS_RATE * across_cols(surface) + rotation * current[2])
    north_new = mask_keep * (current[2] - PRESS_RATE * across_rows(surface) - rotation * current[1])
    return jnp.stack([height, east_new, north_new])

def run_slice(initial, slice_index, sea_mask, depth_field, drag_rate, tide_cos, tide_sin):
    retain = 1.0 / (1.0 + drag_rate)
    rotation = coriolis(sea_mask.shape[0])
    current = initial * sea_mask
    phase_unit = 2.0 * math.pi / (SLICES * STEPS)
    for step_number in range(STEPS):
        phase_now = (slice_index * STEPS + step_number).astype(jnp.float32) * phase_unit
        forcing = jnp.cos(phase_now) * tide_cos + jnp.sin(phase_now) * tide_sin
        current = advance(current, sea_mask, depth_field, retain, forcing, rotation)
    return current

def reference(start_states, ocean_mask, depth_class, class_depth, drag_rate, tide_cos, tide_sin):
    sea_mask = ocean_mask.astype(jnp.float32)
    classes = jnp.arange(NCLASS, dtype=jnp.int32)
    depth_field = lax.optimization_barrier(jnp.sum(jnp.where(depth_class[..., None] == classes, class_depth, jnp.zeros_like(class_depth)), axis=-1))
    indices = jnp.arange(SLICES, dtype=jnp.int32)

    def forward(operands):
        initial, slice_index = operands
        return run_slice(initial, slice_index, sea_mask, depth_field, drag_rate, tide_cos, tide_sin)
    end_states = lax.map(forward, (start_states, indices))
    defect = sea_mask * (end_states - jnp.roll(start_states, -1, axis=0))

    def backward(operands):
        initial, slice_index, weight = operands

        def slice_map(start_in, drag_in):
            return run_slice(start_in, slice_index, sea_mask, depth_field, drag_in, tide_cos, tide_sin)
        _, pull_back = jax.vjp(slice_map, initial, drag_rate)
        return pull_back(weight)
    pulled, drag_terms = lax.map(backward, (start_states, indices, defect))
    state_grad = pulled - jnp.roll(defect, 1, axis=0)
    drag_grad = lax.optimization_barrier(jnp.sum(drag_terms, axis=0)) / SLICES
    return (defect, state_grad, drag_grad)
```

```python
import math

import jax
import jax.numpy as jnp
from jax import lax
from jax.sharding import PartitionSpec as P

STEPS = 8


FLUX_RATE = 0.7
PRESS_RATE = 0.7
ROTATION_RATE = 0.15


def ring_pairs(count, steps):
    return [(source, (source + steps) % count) for source in range(count)]


def with_halo(block, axis, width):
    count = lax.axis_size(axis)
    low = lax.ppermute(block[..., block.shape[-1] - width :], axis, ring_pairs(count, 1))
    high = lax.ppermute(block[..., :width], axis, ring_pairs(count, -1))
    return jnp.concatenate([low, block, high], axis=-1)


def from_behind(value, axis, steps):
    return lax.ppermute(value, axis, ring_pairs(lax.axis_size(axis), steps))


def cropped(values_in, cut_width):
    if cut_width == 0:
        return values_in
    return values_in[..., cut_width : values_in.shape[-1] - cut_width]


def across_cols(values_in):
    return 0.5 * (values_in[..., 2:] - values_in[..., :-2])


def across_rows(values_in):
    zeros_row = jnp.zeros_like(values_in[..., :1, :])
    upper_rows = jnp.concatenate([values_in[..., 1:, :], zeros_row], axis=-2)
    lower_rows = jnp.concatenate([zeros_row, values_in[..., :-1, :]], axis=-2)
    return 0.5 * (upper_rows - lower_rows)


def coriolis(rows_count):
    latitude = math.pi * ((jnp.arange(rows_count, dtype=jnp.float32) + 0.5) / rows_count - 0.5)
    return (ROTATION_RATE * jnp.sin(latitude))[:, None]


def advance_wide(current, statics, rotation, cosine, sine_now):
    sea_mask, depth_field, retain = (statics[0], statics[1], statics[2])
    height, east_vel, north_vel = (current[0], current[1], current[2])
    spread = across_cols(depth_field * east_vel) + cropped(across_rows(depth_field * north_vel), 1)
    height_new = cropped(sea_mask, 1) * (cropped(height, 1) - FLUX_RATE * spread)
    surface = height_new + cropped(cosine * statics[3] + sine_now * statics[4], 1)
    mask_keep = cropped(sea_mask * retain, 2)
    east_mid = cropped(east_vel, 2)
    north_mid = cropped(north_vel, 2)
    east_new = mask_keep * (east_mid - PRESS_RATE * across_cols(surface) + rotation * north_mid)
    north_new = mask_keep * (
        north_mid - PRESS_RATE * cropped(across_rows(surface), 1) - rotation * east_mid
    )
    return jnp.stack([cropped(height_new, 1), east_new, north_new])


def adjoint_step(adjoint, statics, rotation):
    sea_mask, depth_field, retain = (statics[0], statics[1], statics[2])
    mask_keep = sea_mask * retain
    east_part = mask_keep * adjoint[1]
    north_part = mask_keep * adjoint[2]
    summed = cropped(adjoint[0], 1) + PRESS_RATE * (
        across_cols(east_part) + cropped(across_rows(north_part), 1)
    )
    height_part = cropped(sea_mask, 1) * summed
    depth_flux = FLUX_RATE * cropped(depth_field, 2)
    east_in = (
        cropped(east_part, 2)
        - rotation * cropped(north_part, 2)
        + depth_flux * across_cols(height_part)
    )
    north_in = (
        cropped(north_part, 2)
        + rotation * cropped(east_part, 2)
        + depth_flux * cropped(across_rows(height_part), 1)
    )
    return (jnp.stack([cropped(height_part, 1), east_in, north_in]), east_part, north_part)


def reduce_scatter_rows(value, axis):
    count = lax.axis_size(axis)
    bits = count.bit_length() - 1
    me = lax.axis_index(axis)
    rows = value.shape[0] // count
    buf = value.reshape((2,) * bits + (rows, value.shape[1]))
    for bit in range(bits):
        at = bits - 1 - bit
        mine = ((me >> bit) & 1) == 1
        low = lax.index_in_dim(buf, 0, axis=at, keepdims=False)
        high = lax.index_in_dim(buf, 1, axis=at, keepdims=False)
        keep = jnp.where(mine, high, low)
        send = jnp.where(mine, low, high)
        pairs = [(source, source ^ (1 << bit)) for source in range(count)]
        buf = keep + lax.ppermute(send, axis, pairs)
    return buf


def local(start_states, ocean_mask, depth_class, class_depth, drag_rate, tide_cos, tide_sin):
    halo = 2 * STEPS
    slice_count = lax.axis_size("tm")
    slice_index = lax.axis_index("tm")
    sea_mask = ocean_mask.astype(jnp.float32)
    classes = jnp.arange(class_depth.shape[0], dtype=jnp.int32)
    depth_field = jnp.sum(
        jnp.where(depth_class[None] == classes[:, None, None], class_depth[:, None, None], 0.0),
        axis=0,
    )
    retain = 1.0 / (1.0 + drag_rate)
    initial = start_states[0]
    following = from_behind(initial, "tm", -1)
    wide = with_halo(
        jnp.concatenate(
            [initial, jnp.stack([sea_mask, depth_field, retain, tide_cos, tide_sin])], axis=0
        ),
        "cell",
        halo,
    )
    statics = wide[3:]
    rotation = coriolis(sea_mask.shape[0])
    current = wide[:3] * statics[0]
    phase_unit = 2.0 * math.pi / (slice_count * STEPS)
    stored = []
    for step_number in range(STEPS):
        phase_now = (slice_index * STEPS + step_number).astype(jnp.float32) * phase_unit
        current = advance_wide(
            current, cropped(statics, 2 * step_number), rotation, jnp.cos(phase_now), jnp.sin(phase_now)
        )
        stored.append(cropped(current[1:], halo - 2 * (step_number + 1)))
    defect = sea_mask * (current - following)
    behind = from_behind(defect, "tm", 1)
    adjoint = with_halo(defect, "cell", halo)
    drag_total = jnp.zeros_like(drag_rate)
    for back in range(STEPS):
        step_number = STEPS - 1 - back
        margin = halo - 2 * back
        adjoint, east_part, north_part = adjoint_step(adjoint, cropped(statics, 2 * back), rotation)
        outputs = stored[step_number]
        drag_total = drag_total - (
            cropped(east_part, margin) * outputs[0] + cropped(north_part, margin) * outputs[1]
        )
    state_grad = sea_mask * adjoint - behind
    drag_grad = reduce_scatter_rows(drag_total, "tm") / slice_count
    return (defect[None], state_grad[None], drag_grad)


def solution(mesh):
    return jax.shard_map(
        local,
        mesh=mesh,
        in_specs=(
            P("tm", None, None, "cell"),
            P(None, "cell"),
            P(None, "cell"),
            P(),
            P(None, "cell"),
            P(None, "cell"),
            P(None, "cell"),
        ),
        out_specs=(P("tm", None, None, "cell"), P("tm", None, None, "cell"), P("tm", "cell")),
        check_vma=False,
    )
```

```python
import math

import jax
import jax.numpy as jnp
from jax import lax
from jax.sharding import PartitionSpec as P

STEPS = 8


FLUX_RATE = 0.7
PRESS_RATE = 0.7
ROTATION_RATE = 0.15


def ring_pairs(count, steps):
    return [(source, (source + steps) % count) for source in range(count)]


def grid_pairs(slices, cells, slice_steps, cell_steps):
    return [
        (t * cells + c, ((t + slice_steps) % slices) * cells + (c + cell_steps) % cells)
        for t in range(slices)
        for c in range(cells)
    ]


def lane_dense(strip):
    return jnp.swapaxes(strip, -1, -2)


def from_behind(value, axis, steps):
    return lax.ppermute(value, axis, ring_pairs(lax.axis_size(axis), steps))


def cropped(values_in, cut_width):
    if cut_width == 0:
        return values_in
    return values_in[..., cut_width : values_in.shape[-1] - cut_width]


def across_cols(values_in):
    return 0.5 * (values_in[..., 2:] - values_in[..., :-2])


def across_rows(values_in):
    zeros_row = jnp.zeros_like(values_in[..., :1, :])
    upper_rows = jnp.concatenate([values_in[..., 1:, :], zeros_row], axis=-2)
    lower_rows = jnp.concatenate([zeros_row, values_in[..., :-1, :]], axis=-2)
    return 0.5 * (upper_rows - lower_rows)


def coriolis(rows_count):
    latitude = math.pi * ((jnp.arange(rows_count, dtype=jnp.float32) + 0.5) / rows_count - 0.5)
    return (ROTATION_RATE * jnp.sin(latitude))[:, None]


def advance_wide(current, statics, rotation, cosine, sine_now):
    sea_mask, depth_field, retain = (statics[0], statics[1], statics[2])
    height, east_vel, north_vel = (current[0], current[1], current[2])
    spread = across_cols(depth_field * east_vel) + cropped(across_rows(depth_field * north_vel), 1)
    height_new = cropped(sea_mask, 1) * (cropped(height, 1) - FLUX_RATE * spread)
    surface = height_new + cropped(cosine * statics[3] + sine_now * statics[4], 1)
    mask_keep = cropped(sea_mask * retain, 2)
    east_mid = cropped(east_vel, 2)
    north_mid = cropped(north_vel, 2)
    east_new = mask_keep * (east_mid - PRESS_RATE * across_cols(surface) + rotation * north_mid)
    north_new = mask_keep * (
        north_mid - PRESS_RATE * cropped(across_rows(surface), 1) - rotation * east_mid
    )
    return jnp.stack([cropped(height_new, 1), east_new, north_new])


def adjoint_step(adjoint, statics, rotation):
    sea_mask, depth_field, retain = (statics[0], statics[1], statics[2])
    mask_keep = sea_mask * retain
    east_part = mask_keep * adjoint[1]
    north_part = mask_keep * adjoint[2]
    summed = cropped(adjoint[0], 1) + PRESS_RATE * (
        across_cols(east_part) + cropped(across_rows(north_part), 1)
    )
    height_part = cropped(sea_mask, 1) * summed
    depth_flux = FLUX_RATE * cropped(depth_field, 2)
    east_in = (
        cropped(east_part, 2)
        - rotation * cropped(north_part, 2)
        + depth_flux * across_cols(height_part)
    )
    north_in = (
        cropped(north_part, 2)
        + rotation * cropped(east_part, 2)
        + depth_flux * cropped(across_rows(height_part), 1)
    )
    return (jnp.stack([cropped(height_part, 1), east_in, north_in]), east_part, north_part)


def reduce_scatter_rows(value, axis):
    count = lax.axis_size(axis)
    pieces = value.reshape((count, value.shape[0] // count, value.shape[1]))
    return jnp.sum(lax.all_to_all(pieces, axis, 0, 0, tiled=True), axis=0)


def local(start_states, ocean_mask, depth_class, class_depth, drag_rate, tide_cos, tide_sin):
    halo = 2 * STEPS
    slice_count = lax.axis_size("tm")
    slice_index = lax.axis_index("tm")
    sea_mask = ocean_mask.astype(jnp.float32)
    classes = jnp.arange(class_depth.shape[0], dtype=jnp.int32)
    depth_field = jnp.sum(
        jnp.where(depth_class[None] == classes[:, None, None], class_depth[:, None, None], 0.0),
        axis=0,
    )
    retain = 1.0 / (1.0 + drag_rate)
    initial = start_states[0]
    slices, cells = slice_count, lax.axis_size("cell")
    own = jnp.concatenate(
        [initial, jnp.stack([sea_mask, depth_field, retain, tide_cos, tide_sin])], axis=0
    )
    width = own.shape[-1]
    grid = ("tm", "cell")
    from_left = lax.ppermute(lane_dense(own[..., width - 2 * halo :]), "cell", ring_pairs(cells, 1))
    from_right = lax.ppermute(lane_dense(own[..., : 2 * halo]), "cell", ring_pairs(cells, -1))
    next_left = lax.ppermute(
        lane_dense(initial[..., width - halo :]), grid, grid_pairs(slices, cells, -1, 1)
    )
    next_right = lax.ppermute(lane_dense(initial[..., :halo]), grid, grid_pairs(slices, cells, -1, -1))
    following = from_behind(initial, "tm", -1)
    wide = jnp.concatenate([lane_dense(from_left), own, lane_dense(from_right)], axis=-1)
    statics = wide[3:]
    following = jnp.concatenate([lane_dense(next_left), following, lane_dense(next_right)], axis=-1)
    rotation = coriolis(sea_mask.shape[0])
    current = wide[:3] * statics[0]
    phase_unit = 2.0 * math.pi / (slice_count * STEPS)
    stored = []
    for step_number in range(STEPS):
        phase_now = (slice_index * STEPS + step_number).astype(jnp.float32) * phase_unit
        current = advance_wide(
            current, cropped(statics, 2 * step_number), rotation, jnp.cos(phase_now), jnp.sin(phase_now)
        )
        stored.append(cropped(current[1:], 2 * halo - 2 * (step_number + 1)))
    adjoint = cropped(statics[0], halo) * (current - following)
    defect = cropped(adjoint, halo)
    behind = from_behind(defect, "tm", 1)
    drag_total = jnp.zeros_like(drag_rate)
    for back in range(STEPS):
        step_number = STEPS - 1 - back
        margin = halo - 2 * back
        adjoint, east_part, north_part = adjoint_step(
            adjoint, cropped(statics, halo + 2 * back), rotation
        )
        outputs = stored[step_number]
        drag_total = drag_total - (
            cropped(east_part, margin) * outputs[0] + cropped(north_part, margin) * outputs[1]
        )
    state_grad = sea_mask * adjoint - behind
    drag_grad = reduce_scatter_rows(drag_total, "tm") / slice_count
    return (defect[None], state_grad[None], drag_grad)


def solution(mesh):
    return jax.shard_map(
        local,
        mesh=mesh,
        in_specs=(
            P("tm", None, None, "cell"),
            P(None, "cell"),
            P(None, "cell"),
            P(),
            P(None, "cell"),
            P(None, "cell"),
            P(None, "cell"),
        ),
        out_specs=(P("tm", None, None, "cell"), P("tm", None, None, "cell"), P("tm", "cell")),
        check_vma=False,
    )
```

```python
import math

import jax
import jax.numpy as jnp
from jax import lax
from jax.sharding import PartitionSpec as P

STEPS = 8


FLUX_RATE = 0.7
PRESS_RATE = 0.7
ROTATION_RATE = 0.15


def ring_pairs(count, steps):
    return [(source, (source + steps) % count) for source in range(count)]


def lane_dense(strip):
    return jnp.swapaxes(strip, -1, -2)


def from_behind(value, axis, steps):
    return lax.ppermute(value, axis, ring_pairs(lax.axis_size(axis), steps))


def cropped(values_in, cut_width):
    if cut_width == 0:
        return values_in
    return values_in[..., cut_width : values_in.shape[-1] - cut_width]


def across_cols(values_in):
    return 0.5 * (values_in[..., 2:] - values_in[..., :-2])


def across_rows(values_in):
    zeros_row = jnp.zeros_like(values_in[..., :1, :])
    upper_rows = jnp.concatenate([values_in[..., 1:, :], zeros_row], axis=-2)
    lower_rows = jnp.concatenate([zeros_row, values_in[..., :-1, :]], axis=-2)
    return 0.5 * (upper_rows - lower_rows)


def coriolis(rows_count):
    latitude = math.pi * ((jnp.arange(rows_count, dtype=jnp.float32) + 0.5) / rows_count - 0.5)
    return (ROTATION_RATE * jnp.sin(latitude))[:, None]


def advance_wide(current, statics, rotation, cosine, sine_now):
    sea_mask, depth_field, retain = (statics[0], statics[1], statics[2])
    height, east_vel, north_vel = (current[0], current[1], current[2])
    spread = across_cols(depth_field * east_vel) + cropped(across_rows(depth_field * north_vel), 1)
    height_new = cropped(sea_mask, 1) * (cropped(height, 1) - FLUX_RATE * spread)
    surface = height_new + cropped(cosine * statics[3] + sine_now * statics[4], 1)
    mask_keep = cropped(sea_mask * retain, 2)
    east_mid = cropped(east_vel, 2)
    north_mid = cropped(north_vel, 2)
    east_new = mask_keep * (east_mid - PRESS_RATE * across_cols(surface) + rotation * north_mid)
    north_new = mask_keep * (
        north_mid - PRESS_RATE * cropped(across_rows(surface), 1) - rotation * east_mid
    )
    return jnp.stack([cropped(height_new, 1), east_new, north_new])


def adjoint_step(adjoint, statics, rotation):
    sea_mask, depth_field, retain = (statics[0], statics[1], statics[2])
    mask_keep = sea_mask * retain
    east_part = mask_keep * adjoint[1]
    north_part = mask_keep * adjoint[2]
    summed = cropped(adjoint[0], 1) + PRESS_RATE * (
        across_cols(east_part) + cropped(across_rows(north_part), 1)
    )
    height_part = cropped(sea_mask, 1) * summed
    depth_flux = FLUX_RATE * cropped(depth_field, 2)
    east_in = (
        cropped(east_part, 2)
        - rotation * cropped(north_part, 2)
        + depth_flux * across_cols(height_part)
    )
    north_in = (
        cropped(north_part, 2)
        + rotation * cropped(east_part, 2)
        + depth_flux * cropped(across_rows(height_part), 1)
    )
    return (jnp.stack([cropped(height_part, 1), east_in, north_in]), east_part, north_part)


def reduce_scatter_rows(value, axis):
    count = lax.axis_size(axis)
    pieces = value.reshape((count, value.shape[0] // count, value.shape[1]))
    return jnp.sum(lax.all_to_all(pieces, axis, 0, 0, tiled=True), axis=0)


def local(start_states, ocean_mask, depth_class, class_depth, drag_rate, tide_cos, tide_sin):
    halo = 2 * STEPS
    slice_count = lax.axis_size("tm")
    slice_index = lax.axis_index("tm")
    sea_mask = ocean_mask.astype(jnp.float32)
    classes = jnp.arange(class_depth.shape[0], dtype=jnp.int32)
    depth_field = jnp.sum(
        jnp.where(depth_class[None] == classes[:, None, None], class_depth[:, None, None], 0.0),
        axis=0,
    )
    retain = 1.0 / (1.0 + drag_rate)
    initial = start_states[0]
    slices, cells = slice_count, lax.axis_size("cell")
    own = jnp.concatenate(
        [initial, jnp.stack([sea_mask, depth_field, retain, tide_cos, tide_sin])], axis=0
    )
    width = own.shape[-1]
    following = from_behind(initial, "tm", -1)
    fields, lanes = own.shape[0], own.shape[1]

    def strips(at_right):
        mine = own[..., width - 2 * halo :] if at_right else own[..., : 2 * halo]
        theirs = following[..., width - halo :] if at_right else following[..., :halo]
        return jnp.concatenate(
            [lane_dense(mine).reshape(-1, lanes), lane_dense(theirs).reshape(-1, lanes)], axis=0
        )

    def unpacked(packed):
        mine = lane_dense(packed[: fields * 2 * halo].reshape(fields, 2 * halo, lanes))
        theirs = lane_dense(packed[fields * 2 * halo :].reshape(3, halo, lanes))
        return mine, theirs

    left_own, left_next = unpacked(lax.ppermute(strips(True), "cell", ring_pairs(cells, 1)))
    right_own, right_next = unpacked(lax.ppermute(strips(False), "cell", ring_pairs(cells, -1)))
    wide = jnp.concatenate([left_own, own, right_own], axis=-1)
    statics = wide[3:]
    following = jnp.concatenate([left_next, following, right_next], axis=-1)
    rotation = coriolis(sea_mask.shape[0])
    current = wide[:3] * statics[0]
    phase_unit = 2.0 * math.pi / (slice_count * STEPS)
    stored = []
    for step_number in range(STEPS):
        phase_now = (slice_index * STEPS + step_number).astype(jnp.float32) * phase_unit
        current = advance_wide(
            current, cropped(statics, 2 * step_number), rotation, jnp.cos(phase_now), jnp.sin(phase_now)
        )
        stored.append(cropped(current[1:], 2 * halo - 2 * (step_number + 1)))
    adjoint = cropped(statics[0], halo) * (current - following)
    defect = cropped(adjoint, halo)
    behind = from_behind(defect, "tm", 1)
    drag_total = jnp.zeros_like(drag_rate)
    for back in range(STEPS):
        step_number = STEPS - 1 - back
        margin = halo - 2 * back
        adjoint, east_part, north_part = adjoint_step(
            adjoint, cropped(statics, halo + 2 * back), rotation
        )
        outputs = stored[step_number]
        drag_total = drag_total - (
            cropped(east_part, margin) * outputs[0] + cropped(north_part, margin) * outputs[1]
        )
    state_grad = sea_mask * adjoint - behind
    drag_grad = reduce_scatter_rows(drag_total, "tm") / slice_count
    return (defect[None], state_grad[None], drag_grad)


def solution(mesh):
    return jax.shard_map(
        local,
        mesh=mesh,
        in_specs=(
            P("tm", None, None, "cell"),
            P(None, "cell"),
            P(None, "cell"),
            P(),
            P(None, "cell"),
            P(None, "cell"),
            P(None, "cell"),
        ),
        out_specs=(P("tm", None, None, "cell"), P("tm", None, None, "cell"), P("tm", "cell")),
        check_vma=False,
    )
```

```python
import math

import jax
import jax.numpy as jnp
from jax import lax
from jax.experimental import pallas as pl
from jax.experimental.pallas import tpu as pltpu
from jax.sharding import PartitionSpec as P

STEPS = 8


FLUX_RATE = 0.7
PRESS_RATE = 0.7
ROTATION_RATE = 0.15


def ring_pairs(count, steps):
    return [(source, (source + steps) % count) for source in range(count)]


def lane_dense(strip):
    return jnp.swapaxes(strip, -1, -2)


def from_behind(value, axis, steps):
    return lax.ppermute(value, axis, ring_pairs(lax.axis_size(axis), steps))


def coriolis(rows_count):
    latitude = math.pi * ((jnp.arange(rows_count, dtype=jnp.float32) + 0.5) / rows_count - 0.5)
    return (ROTATION_RATE * jnp.sin(latitude))[:, None]


def shooting_kernel(trig_ref, rot_ref, wide_ref, next_ref, defect_ref, pulled_ref, drag_ref, stored_ref):
    rows, lanes = wide_ref.shape[-2], wide_ref.shape[-1]
    tile = defect_ref.shape[-1]
    row = lax.broadcasted_iota(jnp.int32, (rows, lanes), 0)
    first, last = row == 0, row == rows - 1

    def across_cols(q):
        return 0.5 * (pltpu.roll(q, lanes - 1, 1) - pltpu.roll(q, 1, 1))

    def across_rows(q):
        upper = jnp.where(last, 0.0, pltpu.roll(q, rows - 1, 0))
        lower = jnp.where(first, 0.0, pltpu.roll(q, 1, 0))
        return 0.5 * (upper - lower)

    sea, depth, retain = wide_ref[3], wide_ref[4], wide_ref[5]
    rot = rot_ref[...]
    keep = sea * retain
    height, east, north = wide_ref[0] * sea, wide_ref[1] * sea, wide_ref[2] * sea
    for step in range(STEPS):
        force = trig_ref[step] * wide_ref[6] + trig_ref[STEPS + step] * wide_ref[7]
        spread = across_cols(depth * east) + across_rows(depth * north)
        height = sea * (height - FLUX_RATE * spread)
        surface = height + force
        east, north = (
            keep * (east - PRESS_RATE * across_cols(surface) + rot * north),
            keep * (north - PRESS_RATE * across_rows(surface) - rot * east),
        )
        stored_ref[step, 0] = east[:, :tile]
        stored_ref[step, 1] = north[:, :tile]
    height = sea * (height - next_ref[0])
    east = sea * (east - next_ref[1])
    north = sea * (north - next_ref[2])
    defect_ref[0] = height[:, :tile]
    defect_ref[1] = east[:, :tile]
    defect_ref[2] = north[:, :tile]
    depth_flux = FLUX_RATE * depth
    drag = jnp.zeros((rows, tile), jnp.float32)
    for back in range(STEPS):
        step = STEPS - 1 - back
        east_part = keep * east
        north_part = keep * north
        height = sea * (height + PRESS_RATE * (across_cols(east_part) + across_rows(north_part)))
        east = east_part - rot * north_part + depth_flux * across_cols(height)
        north = north_part + rot * east_part + depth_flux * across_rows(height)
        drag = drag - (
            east_part[:, :tile] * stored_ref[step, 0] + north_part[:, :tile] * stored_ref[step, 1]
        )
    sea_tile = sea[:, :tile]
    pulled_ref[0] = sea_tile * height[:, :tile]
    pulled_ref[1] = sea_tile * east[:, :tile]
    pulled_ref[2] = sea_tile * north[:, :tile]
    drag_ref[...] = drag


def shooting(trig, rotation, wide, following, tile):
    rows, lanes = wide.shape[-2], wide.shape[-1]
    vmem = pl.BlockSpec(memory_space=pltpu.VMEM)
    state = jax.ShapeDtypeStruct((3, rows, tile), jnp.float32)
    return pl.pallas_call(
        shooting_kernel,
        out_shape=(state, state, jax.ShapeDtypeStruct((rows, tile), jnp.float32)),
        in_specs=[pl.BlockSpec(memory_space=pltpu.SMEM), vmem, vmem, vmem],
        out_specs=(vmem, vmem, vmem),
        scratch_shapes=[pltpu.VMEM((STEPS, 2, rows, tile), jnp.float32)],
        cost_estimate=pl.CostEstimate(
            flops=2 * STEPS * 60 * rows * lanes, transcendentals=0, bytes_accessed=4 * rows * (11 * lanes + 7 * tile)
        ),
    )(trig, rotation, wide, following)


def reduce_scatter_rows(value, axis):
    count = lax.axis_size(axis)
    pieces = value.reshape((count, value.shape[0] // count, value.shape[1]))
    return jnp.sum(lax.all_to_all(pieces, axis, 0, 0, tiled=True), axis=0)


def local(start_states, ocean_mask, depth_class, class_depth, drag_rate, tide_cos, tide_sin):
    halo = 2 * STEPS
    slice_count = lax.axis_size("tm")
    slice_index = lax.axis_index("tm")
    sea_mask = ocean_mask.astype(jnp.float32)
    classes = jnp.arange(class_depth.shape[0], dtype=jnp.int32)
    depth_field = jnp.sum(
        jnp.where(depth_class[None] == classes[:, None, None], class_depth[:, None, None], 0.0),
        axis=0,
    )
    retain = 1.0 / (1.0 + drag_rate)
    initial = start_states[0]
    cells = lax.axis_size("cell")
    own = jnp.concatenate(
        [initial, jnp.stack([sea_mask, depth_field, retain, tide_cos, tide_sin])], axis=0
    )
    fields, rows, width = own.shape
    following = from_behind(initial, "tm", -1)

    def strips(at_right):
        mine = own[..., width - 2 * halo :] if at_right else own[..., : 2 * halo]
        theirs = following[..., width - halo :] if at_right else following[..., :halo]
        return jnp.concatenate(
            [lane_dense(mine).reshape(-1, rows), lane_dense(theirs).reshape(-1, rows)], axis=0
        )

    def unpacked(packed):
        mine = lane_dense(packed[: fields * 2 * halo].reshape(fields, 2 * halo, rows))
        theirs = lane_dense(packed[fields * 2 * halo :].reshape(3, halo, rows))
        return mine, theirs

    left_own, left_next = unpacked(lax.ppermute(strips(True), "cell", ring_pairs(cells, 1)))
    right_own, right_next = unpacked(lax.ppermute(strips(False), "cell", ring_pairs(cells, -1)))
    lanes = 2 * width

    def circular(middle, right, left):
        gap = jnp.zeros(middle.shape[:-1] + (lanes - width - right.shape[-1] - left.shape[-1],), middle.dtype)
        return jnp.concatenate([middle, right, gap, left], axis=-1)

    phase_unit = 2.0 * math.pi / (slice_count * STEPS)
    phases = (slice_index * STEPS + jnp.arange(STEPS)).astype(jnp.float32) * phase_unit
    trig = jnp.concatenate([jnp.cos(phases), jnp.sin(phases)])
    defect, pulled, drag_total = shooting(
        trig,
        coriolis(rows),
        circular(own, right_own, left_own),
        circular(following, right_next, left_next),
        width,
    )
    behind = from_behind(defect, "tm", 1)
    state_grad = pulled - behind
    drag_grad = reduce_scatter_rows(drag_total, "tm") / slice_count
    return (defect[None], state_grad[None], drag_grad)


def solution(mesh):
    return jax.shard_map(
        local,
        mesh=mesh,
        in_specs=(
            P("tm", None, None, "cell"),
            P(None, "cell"),
            P(None, "cell"),
            P(),
            P(None, "cell"),
            P(None, "cell"),
            P(None, "cell"),
        ),
        out_specs=(P("tm", None, None, "cell"), P("tm", None, None, "cell"), P("tm", "cell")),
        check_vma=False,
    )
```

```python
import functools
import math

import jax
import jax.numpy as jnp
from jax import lax
from jax.experimental import pallas as pl
from jax.experimental.pallas import tpu as pltpu
from jax.sharding import PartitionSpec as P

STEPS = 8


FLUX_RATE = 0.7
PRESS_RATE = 0.7
ROTATION_RATE = 0.15


def ring_pairs(count, steps):
    return [(source, (source + steps) % count) for source in range(count)]


def lane_dense(strip):
    return jnp.swapaxes(strip, -1, -2)


def from_behind(value, axis, steps):
    return lax.ppermute(value, axis, ring_pairs(lax.axis_size(axis), steps))


def coriolis(rows_count):
    latitude = math.pi * ((jnp.arange(rows_count, dtype=jnp.float32) + 0.5) / rows_count - 0.5)
    return (ROTATION_RATE * jnp.sin(latitude))[:, None]


def shooting_kernel(
    trig_ref, rot_ref, own_ref, next_ref, left_ref, right_ref,
    defect_ref, pulled_ref, drag_ref, wide_ref, ahead_ref, stored_ref, *, halo, scale
):
    rows, tile = own_ref.shape[-2], own_ref.shape[-1]
    lanes = wide_ref.shape[-1]

    def circular(middle, right, left):
        gap = jnp.zeros((tile - right.shape[0] - left.shape[0], rows), jnp.float32)
        rim = jnp.transpose(jnp.concatenate([right, gap, left], axis=0))
        return jnp.concatenate([middle, rim], axis=1)

    fields = own_ref.shape[0]
    wide = 2 * halo
    for field in range(fields):
        strip = slice(field * wide, (field + 1) * wide)
        wide_ref[field] = circular(own_ref[field], right_ref[strip, :], left_ref[strip, :])
    for field in range(next_ref.shape[0]):
        strip = slice(fields * wide + field * halo, fields * wide + (field + 1) * halo)
        ahead_ref[field] = circular(next_ref[field], right_ref[strip, :], left_ref[strip, :])

    row = lax.broadcasted_iota(jnp.int32, (rows, lanes), 0)
    first, last = row == 0, row == rows - 1
    def across_cols(q):
        return 0.5 * (pltpu.roll(q, lanes - 1, 1) - pltpu.roll(q, 1, 1))

    def across_rows(q):
        upper = jnp.where(last, 0.0, pltpu.roll(q, rows - 1, 0))
        lower = jnp.where(first, 0.0, pltpu.roll(q, 1, 0))
        return 0.5 * (upper - lower)

    sea, depth, retain = wide_ref[3], wide_ref[4], wide_ref[5]
    rot = rot_ref[...]
    keep = sea * retain
    height, east, north = wide_ref[0] * sea, wide_ref[1] * sea, wide_ref[2] * sea
    for step in range(STEPS):
        force = trig_ref[step] * wide_ref[6] + trig_ref[STEPS + step] * wide_ref[7]
        spread = across_cols(depth * east) + across_rows(depth * north)
        height = sea * (height - FLUX_RATE * spread)
        surface = height + force
        east, north = (
            keep * (east - PRESS_RATE * across_cols(surface) + rot * north),
            keep * (north - PRESS_RATE * across_rows(surface) - rot * east),
        )
        stored_ref[step, 0] = east[:, :tile]
        stored_ref[step, 1] = north[:, :tile]
    height = sea * (height - ahead_ref[0])
    east = sea * (east - ahead_ref[1])
    north = sea * (north - ahead_ref[2])
    defect_ref[0] = height[:, :tile]
    defect_ref[1] = east[:, :tile]
    defect_ref[2] = north[:, :tile]
    depth_flux = FLUX_RATE * depth
    drag = jnp.zeros((rows, tile), jnp.float32)
    for back in range(STEPS):
        step = STEPS - 1 - back
        east_part = keep * east
        north_part = keep * north
        height = sea * (height + PRESS_RATE * (across_cols(east_part) + across_rows(north_part)))
        east = east_part - rot * north_part + depth_flux * across_cols(height)
        north = north_part + rot * east_part + depth_flux * across_rows(height)
        drag = drag - (
            east_part[:, :tile] * stored_ref[step, 0] + north_part[:, :tile] * stored_ref[step, 1]
        )
    sea_tile = sea[:, :tile]
    pulled_ref[0] = sea_tile * height[:, :tile]
    pulled_ref[1] = sea_tile * east[:, :tile]
    pulled_ref[2] = sea_tile * north[:, :tile]
    drag_ref[...] = drag * scale


def shooting(trig, rotation, own, following, from_left, from_right, halo, scale):
    fields, rows, tile = own.shape
    vmem = pl.BlockSpec(memory_space=pltpu.VMEM)
    state = jax.ShapeDtypeStruct((3, rows, tile), jnp.float32)
    lanes = 2 * tile
    return pl.pallas_call(
        functools.partial(shooting_kernel, halo=halo, scale=scale),
        out_shape=(state, state, jax.ShapeDtypeStruct((rows, tile), jnp.float32)),
        in_specs=[pl.BlockSpec(memory_space=pltpu.SMEM)] + [vmem] * 5,
        out_specs=(vmem, vmem, vmem),
        scratch_shapes=[
            pltpu.VMEM((fields, rows, lanes), jnp.float32),
            pltpu.VMEM((3, rows, lanes), jnp.float32),
            pltpu.VMEM((STEPS, 2, rows, tile), jnp.float32),
        ],
        cost_estimate=pl.CostEstimate(
            flops=2 * STEPS * 60 * rows * lanes, transcendentals=0, bytes_accessed=4 * rows * 24 * tile
        ),
    )(trig, rotation, own, following, from_left, from_right)


def reduce_scatter_rows(value, axis):
    count = lax.axis_size(axis)
    pieces = value.reshape((count, value.shape[0] // count, value.shape[1]))
    return jnp.sum(lax.all_to_all(pieces, axis, 0, 0, tiled=True), axis=0)


def local(start_states, ocean_mask, depth_class, class_depth, drag_rate, tide_cos, tide_sin):
    halo = 2 * STEPS
    slice_count = lax.axis_size("tm")
    slice_index = lax.axis_index("tm")
    sea_mask = ocean_mask.astype(jnp.float32)
    classes = jnp.arange(class_depth.shape[0], dtype=jnp.int32)
    depth_field = jnp.sum(
        jnp.where(depth_class[None] == classes[:, None, None], class_depth[:, None, None], 0.0),
        axis=0,
    )
    retain = 1.0 / (1.0 + drag_rate)
    initial = start_states[0]
    cells = lax.axis_size("cell")
    own = jnp.concatenate(
        [initial, jnp.stack([sea_mask, depth_field, retain, tide_cos, tide_sin])], axis=0
    )
    fields, rows, width = own.shape
    following = from_behind(initial, "tm", -1)

    def strips(at_right):
        mine = own[..., width - 2 * halo :] if at_right else own[..., : 2 * halo]
        theirs = following[..., width - halo :] if at_right else following[..., :halo]
        return jnp.concatenate(
            [lane_dense(mine).reshape(-1, rows), lane_dense(theirs).reshape(-1, rows)], axis=0
        )

    from_left = lax.ppermute(strips(True), "cell", ring_pairs(cells, 1))
    from_right = lax.ppermute(strips(False), "cell", ring_pairs(cells, -1))
    phase_unit = 2.0 * math.pi / (slice_count * STEPS)
    phases = (slice_index * STEPS + jnp.arange(STEPS)).astype(jnp.float32) * phase_unit
    trig = jnp.concatenate([jnp.cos(phases), jnp.sin(phases)])
    defect, pulled, drag_grad = shooting(
        trig, coriolis(rows), own, following, from_left, from_right, halo, 1.0 / slice_count
    )
    behind = from_behind(defect, "tm", 1)
    state_grad = pulled - behind
    drag_grad = reduce_scatter_rows(drag_grad, "tm")
    return (defect[None], state_grad[None], drag_grad)


def solution(mesh):
    return jax.shard_map(
        local,
        mesh=mesh,
        in_specs=(
            P("tm", None, None, "cell"),
            P(None, "cell"),
            P(None, "cell"),
            P(),
            P(None, "cell"),
            P(None, "cell"),
            P(None, "cell"),
        ),
        out_specs=(P("tm", None, None, "cell"), P("tm", None, None, "cell"), P("tm", "cell")),
        check_vma=False,
    )
```

```python
import functools
import math

import jax
import jax.numpy as jnp
from jax import lax
from jax.experimental import pallas as pl
from jax.experimental.pallas import tpu as pltpu
from jax.sharding import PartitionSpec as P

STEPS = 8


FLUX_RATE = 0.7
PRESS_RATE = 0.7
ROTATION_RATE = 0.15


def ring_pairs(count, steps):
    return [(source, (source + steps) % count) for source in range(count)]


def lane_dense(strip):
    return jnp.swapaxes(strip, -1, -2)


def from_behind(value, axis, steps):
    return lax.ppermute(value, axis, ring_pairs(lax.axis_size(axis), steps))


def coriolis(rows_count):
    latitude = math.pi * ((jnp.arange(rows_count, dtype=jnp.float32) + 0.5) / rows_count - 0.5)
    return (ROTATION_RATE * jnp.sin(latitude))[:, None]


def shooting_kernel(
    trig_ref, rot_ref, own_ref, next_ref, left_ref, right_ref,
    defect_ref, pulled_ref, drag_ref, wide_ref, ahead_ref, stored_ref, *, halo, scale
):
    rows, tile = own_ref.shape[-2], own_ref.shape[-1]
    lanes = wide_ref.shape[-1]

    def circular(middle, right, left):
        gap = jnp.zeros((tile - right.shape[0] - left.shape[0], rows), jnp.float32)
        rim = jnp.transpose(jnp.concatenate([right, gap, left], axis=0))
        return jnp.concatenate([middle, rim], axis=1)

    fields = own_ref.shape[0]
    wide = 2 * halo
    for field in range(fields):
        strip = slice(field * wide, (field + 1) * wide)
        wide_ref[field] = circular(own_ref[field], right_ref[strip, :], left_ref[strip, :])
    for field in range(next_ref.shape[0]):
        strip = slice(fields * wide + field * halo, fields * wide + (field + 1) * halo)
        ahead_ref[field] = circular(next_ref[field], right_ref[strip, :], left_ref[strip, :])

    row = lax.broadcasted_iota(jnp.int32, (rows, lanes), 0)
    first, last = row == 0, row == rows - 1
    def cols_diff(q):
        return pltpu.roll(q, lanes - 1, 1) - pltpu.roll(q, 1, 1)

    def rows_diff(q):
        upper = jnp.where(last, 0.0, pltpu.roll(q, rows - 1, 0))
        lower = jnp.where(first, 0.0, pltpu.roll(q, 1, 0))
        return upper - lower

    half_flux, half_press = 0.5 * FLUX_RATE, 0.5 * PRESS_RATE
    sea, depth, retain = wide_ref[3], wide_ref[4], wide_ref[5]
    rot = rot_ref[...]
    keep = sea * retain
    height, east, north = wide_ref[0] * sea, wide_ref[1] * sea, wide_ref[2] * sea
    for step in range(STEPS):
        force = trig_ref[step] * wide_ref[6] + trig_ref[STEPS + step] * wide_ref[7]
        spread = cols_diff(depth * east) + rows_diff(depth * north)
        height = sea * (height - half_flux * spread)
        surface = height + force
        east, north = (
            keep * (east - half_press * cols_diff(surface) + rot * north),
            keep * (north - half_press * rows_diff(surface) - rot * east),
        )
        stored_ref[step, 0] = east[:, :tile]
        stored_ref[step, 1] = north[:, :tile]
    height = sea * (height - ahead_ref[0])
    east = sea * (east - ahead_ref[1])
    north = sea * (north - ahead_ref[2])
    defect_ref[0] = height[:, :tile]
    defect_ref[1] = east[:, :tile]
    defect_ref[2] = north[:, :tile]
    half_depth_flux = 0.5 * (FLUX_RATE * depth)
    drag = jnp.zeros((rows, tile), jnp.float32)
    for back in range(STEPS):
        step = STEPS - 1 - back
        east_part = keep * east
        north_part = keep * north
        height = sea * (height + half_press * (cols_diff(east_part) + rows_diff(north_part)))
        east = east_part - rot * north_part + half_depth_flux * cols_diff(height)
        north = north_part + rot * east_part + half_depth_flux * rows_diff(height)
        drag = drag - (
            east_part[:, :tile] * stored_ref[step, 0] + north_part[:, :tile] * stored_ref[step, 1]
        )
    sea_tile = sea[:, :tile]
    pulled_ref[0] = sea_tile * height[:, :tile]
    pulled_ref[1] = sea_tile * east[:, :tile]
    pulled_ref[2] = sea_tile * north[:, :tile]
    drag_ref[...] = drag * scale


def shooting(trig, rotation, own, following, from_left, from_right, halo, scale):
    fields, rows, tile = own.shape
    vmem = pl.BlockSpec(memory_space=pltpu.VMEM)
    state = jax.ShapeDtypeStruct((3, rows, tile), jnp.float32)
    lanes = 2 * tile
    return pl.pallas_call(
        functools.partial(shooting_kernel, halo=halo, scale=scale),
        out_shape=(state, state, jax.ShapeDtypeStruct((rows, tile), jnp.float32)),
        in_specs=[pl.BlockSpec(memory_space=pltpu.SMEM)] + [vmem] * 5,
        out_specs=(vmem, vmem, vmem),
        scratch_shapes=[
            pltpu.VMEM((fields, rows, lanes), jnp.float32),
            pltpu.VMEM((3, rows, lanes), jnp.float32),
            pltpu.VMEM((STEPS, 2, rows, tile), jnp.float32),
        ],
        cost_estimate=pl.CostEstimate(
            flops=2 * STEPS * 60 * rows * lanes, transcendentals=0, bytes_accessed=4 * rows * 24 * tile
        ),
    )(trig, rotation, own, following, from_left, from_right)


def reduce_scatter_rows(value, axis):
    count = lax.axis_size(axis)
    pieces = value.reshape((count, value.shape[0] // count, value.shape[1]))
    return jnp.sum(lax.all_to_all(pieces, axis, 0, 0, tiled=True), axis=0)


def local(start_states, ocean_mask, depth_class, class_depth, drag_rate, tide_cos, tide_sin):
    halo = 2 * STEPS
    slice_count = lax.axis_size("tm")
    slice_index = lax.axis_index("tm")
    sea_mask = ocean_mask.astype(jnp.float32)
    classes = jnp.arange(class_depth.shape[0], dtype=jnp.int32)
    depth_field = jnp.sum(
        jnp.where(depth_class[None] == classes[:, None, None], class_depth[:, None, None], 0.0),
        axis=0,
    )
    retain = 1.0 / (1.0 + drag_rate)
    initial = start_states[0]
    cells = lax.axis_size("cell")
    own = jnp.concatenate(
        [initial, jnp.stack([sea_mask, depth_field, retain, tide_cos, tide_sin])], axis=0
    )
    fields, rows, width = own.shape
    following = from_behind(initial, "tm", -1)

    def strips(at_right):
        mine = own[..., width - 2 * halo :] if at_right else own[..., : 2 * halo]
        theirs = following[..., width - halo :] if at_right else following[..., :halo]
        return jnp.concatenate(
            [lane_dense(mine).reshape(-1, rows), lane_dense(theirs).reshape(-1, rows)], axis=0
        )

    from_left = lax.ppermute(strips(True), "cell", ring_pairs(cells, 1))
    from_right = lax.ppermute(strips(False), "cell", ring_pairs(cells, -1))
    phase_unit = 2.0 * math.pi / (slice_count * STEPS)
    phases = (slice_index * STEPS + jnp.arange(STEPS)).astype(jnp.float32) * phase_unit
    trig = jnp.concatenate([jnp.cos(phases), jnp.sin(phases)])
    defect, pulled, drag_grad = shooting(
        trig, coriolis(rows), own, following, from_left, from_right, halo, 1.0 / slice_count
    )
    behind = from_behind(defect, "tm", 1)
    state_grad = pulled - behind
    drag_grad = reduce_scatter_rows(drag_grad, "tm")
    return (defect[None], state_grad[None], drag_grad)


def solution(mesh):
    return jax.shard_map(
        local,
        mesh=mesh,
        in_specs=(
            P("tm", None, None, "cell"),
            P(None, "cell"),
            P(None, "cell"),
            P(),
            P(None, "cell"),
            P(None, "cell"),
            P(None, "cell"),
        ),
        out_specs=(P("tm", None, None, "cell"), P("tm", None, None, "cell"), P("tm", "cell")),
        check_vma=False,
    )
```

```python
import functools
import math

import jax
import jax.numpy as jnp
from jax import lax
from jax.experimental import pallas as pl
from jax.experimental.pallas import tpu as pltpu
from jax.sharding import PartitionSpec as P

STEPS = 8


FLUX_RATE = 0.7
PRESS_RATE = 0.7
ROTATION_RATE = 0.15


def ring_pairs(count, steps):
    return [(source, (source + steps) % count) for source in range(count)]


def lane_dense(strip):
    return jnp.swapaxes(strip, -1, -2)


def from_behind(value, axis, steps):
    return lax.ppermute(value, axis, ring_pairs(lax.axis_size(axis), steps))


def coriolis(rows_count):
    latitude = math.pi * ((jnp.arange(rows_count, dtype=jnp.float32) + 0.5) / rows_count - 0.5)
    return (ROTATION_RATE * jnp.sin(latitude))[:, None]


def shooting_kernel(
    trig_ref, rot_ref, own_ref, next_ref, left_ref, right_ref,
    defect_ref, pulled_ref, drag_ref, wide_ref, ahead_ref, stored_ref, *, halo, scale
):
    rows, tile = own_ref.shape[-2], own_ref.shape[-1]
    span = wide_ref.shape[-2]
    fields = own_ref.shape[0]
    wide = 2 * halo
    for field in range(fields):
        strip = slice(field * wide, (field + 1) * wide)
        wide_ref[field] = jnp.concatenate(
            [left_ref[strip, :], jnp.transpose(own_ref[field]), right_ref[strip, :]], axis=0
        )
    edge = jnp.zeros((halo, rows), jnp.float32)
    for field in range(next_ref.shape[0]):
        strip = slice(fields * wide + field * halo, fields * wide + (field + 1) * halo)
        ahead_ref[field] = jnp.concatenate(
            [edge, left_ref[strip, :], jnp.transpose(next_ref[field]), right_ref[strip, :], edge], axis=0
        )

    lane = lax.broadcasted_iota(jnp.int32, (span, rows), 1)
    first, last = lane == 0, lane == rows - 1
    inner = slice(wide, wide + tile)

    def cols_diff(q):
        return pltpu.roll(q, span - 1, 0) - pltpu.roll(q, 1, 0)

    def rows_diff(q):
        upper = jnp.where(last, 0.0, pltpu.roll(q, rows - 1, 1))
        lower = jnp.where(first, 0.0, pltpu.roll(q, 1, 1))
        return upper - lower

    half_flux, half_press = 0.5 * FLUX_RATE, 0.5 * PRESS_RATE
    sea, depth, retain = wide_ref[3], wide_ref[4], wide_ref[5]
    rot = rot_ref[...]
    keep = sea * retain
    height, east, north = wide_ref[0] * sea, wide_ref[1] * sea, wide_ref[2] * sea
    for step in range(STEPS):
        force = trig_ref[step] * wide_ref[6] + trig_ref[STEPS + step] * wide_ref[7]
        spread = cols_diff(depth * east) + rows_diff(depth * north)
        height = sea * (height - half_flux * spread)
        surface = height + force
        east, north = (
            keep * (east - half_press * cols_diff(surface) + rot * north),
            keep * (north - half_press * rows_diff(surface) - rot * east),
        )
        stored_ref[step, 0] = east[inner]
        stored_ref[step, 1] = north[inner]
    height = sea * (height - ahead_ref[0])
    east = sea * (east - ahead_ref[1])
    north = sea * (north - ahead_ref[2])
    defect_ref[0] = jnp.transpose(height[inner])
    defect_ref[1] = jnp.transpose(east[inner])
    defect_ref[2] = jnp.transpose(north[inner])
    half_depth_flux = 0.5 * (FLUX_RATE * depth)
    drag = jnp.zeros((tile, rows), jnp.float32)
    for back in range(STEPS):
        step = STEPS - 1 - back
        east_part = keep * east
        north_part = keep * north
        height = sea * (height + half_press * (cols_diff(east_part) + rows_diff(north_part)))
        east = east_part - rot * north_part + half_depth_flux * cols_diff(height)
        north = north_part + rot * east_part + half_depth_flux * rows_diff(height)
        drag = drag - (east_part[inner] * stored_ref[step, 0] + north_part[inner] * stored_ref[step, 1])
    sea_tile = sea[inner]
    pulled_ref[0] = jnp.transpose(sea_tile * height[inner])
    pulled_ref[1] = jnp.transpose(sea_tile * east[inner])
    pulled_ref[2] = jnp.transpose(sea_tile * north[inner])
    drag_ref[...] = jnp.transpose(drag * scale)


def shooting(trig, rotation, own, following, from_left, from_right, halo, scale):
    fields, rows, tile = own.shape
    vmem = pl.BlockSpec(memory_space=pltpu.VMEM)
    state = jax.ShapeDtypeStruct((3, rows, tile), jnp.float32)
    span = tile + 4 * halo
    return pl.pallas_call(
        functools.partial(shooting_kernel, halo=halo, scale=scale),
        out_shape=(state, state, jax.ShapeDtypeStruct((rows, tile), jnp.float32)),
        in_specs=[pl.BlockSpec(memory_space=pltpu.SMEM)] + [vmem] * 5,
        out_specs=(vmem, vmem, vmem),
        scratch_shapes=[
            pltpu.VMEM((fields, span, rows), jnp.float32),
            pltpu.VMEM((3, span, rows), jnp.float32),
            pltpu.VMEM((STEPS, 2, tile, rows), jnp.float32),
        ],
        cost_estimate=pl.CostEstimate(
            flops=2 * STEPS * 60 * rows * span, transcendentals=0, bytes_accessed=4 * rows * 24 * tile
        ),
    )(trig, rotation.reshape(1, rows), own, following, from_left, from_right)


def reduce_scatter_rows(value, axis):
    count = lax.axis_size(axis)
    pieces = value.reshape((count, value.shape[0] // count, value.shape[1]))
    return jnp.sum(lax.all_to_all(pieces, axis, 0, 0, tiled=True), axis=0)


def local(start_states, ocean_mask, depth_class, class_depth, drag_rate, tide_cos, tide_sin):
    halo = 2 * STEPS
    slice_count = lax.axis_size("tm")
    slice_index = lax.axis_index("tm")
    sea_mask = ocean_mask.astype(jnp.float32)
    classes = jnp.arange(class_depth.shape[0], dtype=jnp.int32)
    depth_field = jnp.sum(
        jnp.where(depth_class[None] == classes[:, None, None], class_depth[:, None, None], 0.0),
        axis=0,
    )
    retain = 1.0 / (1.0 + drag_rate)
    initial = start_states[0]
    cells = lax.axis_size("cell")
    own = jnp.concatenate(
        [initial, jnp.stack([sea_mask, depth_field, retain, tide_cos, tide_sin])], axis=0
    )
    fields, rows, width = own.shape
    following = from_behind(initial, "tm", -1)

    def strips(at_right):
        mine = own[..., width - 2 * halo :] if at_right else own[..., : 2 * halo]
        theirs = following[..., width - halo :] if at_right else following[..., :halo]
        return jnp.concatenate(
            [lane_dense(mine).reshape(-1, rows), lane_dense(theirs).reshape(-1, rows)], axis=0
        )

    from_left = lax.ppermute(strips(True), "cell", ring_pairs(cells, 1))
    from_right = lax.ppermute(strips(False), "cell", ring_pairs(cells, -1))
    phase_unit = 2.0 * math.pi / (slice_count * STEPS)
    phases = (slice_index * STEPS + jnp.arange(STEPS)).astype(jnp.float32) * phase_unit
    trig = jnp.concatenate([jnp.cos(phases), jnp.sin(phases)])
    defect, pulled, drag_grad = shooting(
        trig, coriolis(rows), own, following, from_left, from_right, halo, 1.0 / slice_count
    )
    behind = from_behind(defect, "tm", 1)
    state_grad = pulled - behind
    drag_grad = reduce_scatter_rows(drag_grad, "tm")
    return (defect[None], state_grad[None], drag_grad)


def solution(mesh):
    return jax.shard_map(
        local,
        mesh=mesh,
        in_specs=(
            P("tm", None, None, "cell"),
            P(None, "cell"),
            P(None, "cell"),
            P(),
            P(None, "cell"),
            P(None, "cell"),
            P(None, "cell"),
        ),
        out_specs=(P("tm", None, None, "cell"), P("tm", None, None, "cell"), P("tm", "cell")),
        check_vma=False,
    )
```

```python
import functools
import math

import jax
import jax.numpy as jnp
from jax import lax
from jax.experimental import pallas as pl
from jax.experimental.pallas import tpu as pltpu
from jax.sharding import PartitionSpec as P

STEPS = 8


FLUX_RATE = 0.7
PRESS_RATE = 0.7
ROTATION_RATE = 0.15


def ring_pairs(count, steps):
    return [(source, (source + steps) % count) for source in range(count)]


def lane_dense(strip):
    return jnp.swapaxes(strip, -1, -2)


def from_behind(value, axis, steps):
    return lax.ppermute(value, axis, ring_pairs(lax.axis_size(axis), steps))


def coriolis(rows_count):
    latitude = math.pi * ((jnp.arange(rows_count, dtype=jnp.float32) + 0.5) / rows_count - 0.5)
    return (ROTATION_RATE * jnp.sin(latitude))[:, None]


def shooting_kernel(
    trig_ref, rot_ref, start_ref, sea_ref, depth_ref, retain_ref, cos_ref, sin_ref, next_ref, left_ref, right_ref,
    defect_ref, pulled_ref, drag_ref, wide_ref, ahead_ref, stored_ref, *, halo, scale
):
    rows, tile = sea_ref.shape[-2], sea_ref.shape[-1]
    span = wide_ref.shape[-2]
    own = [start_ref.at[0], start_ref.at[1], start_ref.at[2], sea_ref, depth_ref, retain_ref, cos_ref, sin_ref]
    fields = len(own)
    wide = 2 * halo
    for field in range(fields):
        strip = slice(field * wide, (field + 1) * wide)
        wide_ref[field] = jnp.concatenate(
            [left_ref[strip, :], jnp.transpose(own[field][...]), right_ref[strip, :]], axis=0
        )
    edge = jnp.zeros((halo, rows), jnp.float32)
    for field in range(next_ref.shape[0]):
        strip = slice(fields * wide + field * halo, fields * wide + (field + 1) * halo)
        ahead_ref[field] = jnp.concatenate(
            [edge, left_ref[strip, :], jnp.transpose(next_ref[field]), right_ref[strip, :], edge], axis=0
        )

    lane = lax.broadcasted_iota(jnp.int32, (span, rows), 1)
    first, last = lane == 0, lane == rows - 1
    inner = slice(wide, wide + tile)

    def cols_diff(q):
        return pltpu.roll(q, span - 1, 0) - pltpu.roll(q, 1, 0)

    def rows_diff(q):
        upper = jnp.where(last, 0.0, pltpu.roll(q, rows - 1, 1))
        lower = jnp.where(first, 0.0, pltpu.roll(q, 1, 1))
        return upper - lower

    half_flux, half_press = 0.5 * FLUX_RATE, 0.5 * PRESS_RATE
    sea, depth, retain = wide_ref[3], wide_ref[4], wide_ref[5]
    rot = rot_ref[...]
    keep = sea * retain
    height, east, north = wide_ref[0] * sea, wide_ref[1] * sea, wide_ref[2] * sea
    for step in range(STEPS):
        force = trig_ref[step] * wide_ref[6] + trig_ref[STEPS + step] * wide_ref[7]
        spread = cols_diff(depth * east) + rows_diff(depth * north)
        height = sea * (height - half_flux * spread)
        surface = height + force
        east, north = (
            keep * (east - half_press * cols_diff(surface) + rot * north),
            keep * (north - half_press * rows_diff(surface) - rot * east),
        )
        stored_ref[step, 0] = east[inner]
        stored_ref[step, 1] = north[inner]
    height = sea * (height - ahead_ref[0])
    east = sea * (east - ahead_ref[1])
    north = sea * (north - ahead_ref[2])
    defect_ref[0] = jnp.transpose(height[inner])
    defect_ref[1] = jnp.transpose(east[inner])
    defect_ref[2] = jnp.transpose(north[inner])
    half_depth_flux = 0.5 * (FLUX_RATE * depth)
    drag = jnp.zeros((tile, rows), jnp.float32)
    for back in range(STEPS):
        step = STEPS - 1 - back
        east_part = keep * east
        north_part = keep * north
        height = sea * (height + half_press * (cols_diff(east_part) + rows_diff(north_part)))
        east = east_part - rot * north_part + half_depth_flux * cols_diff(height)
        north = north_part + rot * east_part + half_depth_flux * rows_diff(height)
        drag = drag - (east_part[inner] * stored_ref[step, 0] + north_part[inner] * stored_ref[step, 1])
    sea_tile = sea[inner]
    pulled_ref[0] = jnp.transpose(sea_tile * height[inner])
    pulled_ref[1] = jnp.transpose(sea_tile * east[inner])
    pulled_ref[2] = jnp.transpose(sea_tile * north[inner])
    drag_ref[...] = jnp.transpose(drag * scale)


def shooting(trig, rotation, start, statics, following, from_left, from_right, halo, scale):
    fields, (rows, tile) = 3 + len(statics), statics[0].shape
    vmem = pl.BlockSpec(memory_space=pltpu.VMEM)
    state = jax.ShapeDtypeStruct((3, rows, tile), jnp.float32)
    span = tile + 4 * halo
    return pl.pallas_call(
        functools.partial(shooting_kernel, halo=halo, scale=scale),
        out_shape=(state, state, jax.ShapeDtypeStruct((rows, tile), jnp.float32)),
        in_specs=[pl.BlockSpec(memory_space=pltpu.SMEM)] + [vmem] * (5 + len(statics)),
        out_specs=(vmem, vmem, vmem),
        scratch_shapes=[
            pltpu.VMEM((fields, span, rows), jnp.float32),
            pltpu.VMEM((3, span, rows), jnp.float32),
            pltpu.VMEM((STEPS, 2, tile, rows), jnp.float32),
        ],
        cost_estimate=pl.CostEstimate(
            flops=2 * STEPS * 60 * rows * span, transcendentals=0, bytes_accessed=4 * rows * 24 * tile
        ),
    )(trig, rotation.reshape(1, rows), start, *statics, following, from_left, from_right)


def reduce_scatter_rows(value, axis):
    count = lax.axis_size(axis)
    pieces = value.reshape((count, value.shape[0] // count, value.shape[1]))
    return jnp.sum(lax.all_to_all(pieces, axis, 0, 0, tiled=True), axis=0)


def local(start_states, ocean_mask, depth_class, class_depth, drag_rate, tide_cos, tide_sin):
    halo = 2 * STEPS
    slice_count = lax.axis_size("tm")
    slice_index = lax.axis_index("tm")
    sea_mask = ocean_mask.astype(jnp.float32)
    classes = jnp.arange(class_depth.shape[0], dtype=jnp.int32)
    depth_field = jnp.sum(
        jnp.where(depth_class[None] == classes[:, None, None], class_depth[:, None, None], 0.0),
        axis=0,
    )
    retain = 1.0 / (1.0 + drag_rate)
    initial = start_states[0]
    cells = lax.axis_size("cell")
    statics = [sea_mask, depth_field, retain, tide_cos, tide_sin]
    own = [initial[0], initial[1], initial[2]] + statics
    rows, width = sea_mask.shape
    following = from_behind(initial, "tm", -1)

    def strips(at_right):
        mine = [field[:, width - 2 * halo :] if at_right else field[:, : 2 * halo] for field in own]
        theirs = following[..., width - halo :] if at_right else following[..., :halo]
        return jnp.concatenate(
            [lane_dense(field) for field in mine] + [lane_dense(theirs).reshape(-1, rows)], axis=0
        )

    from_left = lax.ppermute(strips(True), "cell", ring_pairs(cells, 1))
    from_right = lax.ppermute(strips(False), "cell", ring_pairs(cells, -1))
    phase_unit = 2.0 * math.pi / (slice_count * STEPS)
    phases = (slice_index * STEPS + jnp.arange(STEPS)).astype(jnp.float32) * phase_unit
    trig = jnp.concatenate([jnp.cos(phases), jnp.sin(phases)])
    defect, pulled, drag_grad = shooting(
        trig, coriolis(rows), initial, statics, following, from_left, from_right, halo, 1.0 / slice_count
    )
    behind = from_behind(defect, "tm", 1)
    state_grad = pulled - behind
    drag_grad = reduce_scatter_rows(drag_grad, "tm")
    return (defect[None], state_grad[None], drag_grad)


def solution(mesh):
    return jax.shard_map(
        local,
        mesh=mesh,
        in_specs=(
            P("tm", None, None, "cell"),
            P(None, "cell"),
            P(None, "cell"),
            P(),
            P(None, "cell"),
            P(None, "cell"),
            P(None, "cell"),
        ),
        out_specs=(P("tm", None, None, "cell"), P("tm", None, None, "cell"), P("tm", "cell")),
        check_vma=False,
    )
```

```python
import functools
import math

import jax
import jax.numpy as jnp
from jax import lax
from jax.experimental import pallas as pl
from jax.experimental.pallas import tpu as pltpu
from jax.sharding import PartitionSpec as P

STEPS = 8


FLUX_RATE = 0.7
PRESS_RATE = 0.7
ROTATION_RATE = 0.15


def ring_pairs(count, steps):
    return [(source, (source + steps) % count) for source in range(count)]


def lane_dense(strip):
    return jnp.swapaxes(strip, -1, -2)


def from_behind(value, axis, steps):
    return lax.ppermute(value, axis, ring_pairs(lax.axis_size(axis), steps))


def coriolis(rows_count):
    latitude = math.pi * ((jnp.arange(rows_count, dtype=jnp.float32) + 0.5) / rows_count - 0.5)
    return (ROTATION_RATE * jnp.sin(latitude))[:, None]


def shooting_kernel(
    trig_ref, rot_ref, own_ref, next_ref, left_ref, right_ref,
    defect_ref, pulled_ref, drag_ref, wide_ref, ahead_ref, stored_ref, *, halo, scale
):
    rows, tile = own_ref.shape[-2], own_ref.shape[-1]
    span = wide_ref.shape[-2]
    fields = own_ref.shape[0]
    wide = 2 * halo
    for field in range(fields):
        strip = slice(field * wide, (field + 1) * wide)
        wide_ref[field] = jnp.concatenate(
            [left_ref[strip, :], jnp.transpose(own_ref[field]), right_ref[strip, :]], axis=0
        )
    edge = jnp.zeros((halo, rows), jnp.float32)
    for field in range(next_ref.shape[0]):
        strip = slice(fields * wide + field * halo, fields * wide + (field + 1) * halo)
        ahead_ref[field] = jnp.concatenate(
            [edge, left_ref[strip, :], jnp.transpose(next_ref[field]), right_ref[strip, :], edge], axis=0
        )

    lane = lax.broadcasted_iota(jnp.int32, (span, rows), 1)
    first, last = lane == 0, lane == rows - 1
    inner = slice(wide, wide + tile)

    def cols_diff(q):
        return pltpu.roll(q, span - 1, 0) - pltpu.roll(q, 1, 0)

    def rows_diff(q):
        upper = jnp.where(last, 0.0, pltpu.roll(q, rows - 1, 1))
        lower = jnp.where(first, 0.0, pltpu.roll(q, 1, 1))
        return upper - lower

    half_flux, half_press = 0.5 * FLUX_RATE, 0.5 * PRESS_RATE
    sea, depth, retain = wide_ref[3], wide_ref[4], wide_ref[5]
    rot = rot_ref[...]
    keep = sea * retain
    height, east, north = wide_ref[0] * sea, wide_ref[1] * sea, wide_ref[2] * sea
    for step in range(STEPS):
        force = trig_ref[step] * wide_ref[6] + trig_ref[STEPS + step] * wide_ref[7]
        spread = cols_diff(depth * east) + rows_diff(depth * north)
        height = sea * (height - half_flux * spread)
        surface = height + force
        east, north = (
            keep * (east - half_press * cols_diff(surface) + rot * north),
            keep * (north - half_press * rows_diff(surface) - rot * east),
        )
        stored_ref[step, 0] = east[inner]
        stored_ref[step, 1] = north[inner]
    height = sea * (height - ahead_ref[0])
    east = sea * (east - ahead_ref[1])
    north = sea * (north - ahead_ref[2])
    defect_ref[0] = jnp.transpose(height[inner])
    defect_ref[1] = jnp.transpose(east[inner])
    defect_ref[2] = jnp.transpose(north[inner])
    half_depth_flux = 0.5 * (FLUX_RATE * depth)
    drag = jnp.zeros((tile, rows), jnp.float32)
    for back in range(STEPS):
        step = STEPS - 1 - back
        east_part = keep * east
        north_part = keep * north
        height = sea * (height + half_press * (cols_diff(east_part) + rows_diff(north_part)))
        east = east_part - rot * north_part + half_depth_flux * cols_diff(height)
        north = north_part + rot * east_part + half_depth_flux * rows_diff(height)
        drag = drag - (east_part[inner] * stored_ref[step, 0] + north_part[inner] * stored_ref[step, 1])
    sea_tile = sea[inner]
    pulled_ref[0] = jnp.transpose(sea_tile * height[inner])
    pulled_ref[1] = jnp.transpose(sea_tile * east[inner])
    pulled_ref[2] = jnp.transpose(sea_tile * north[inner])
    drag_ref[...] = jnp.transpose(drag * scale)


def shooting(trig, rotation, own, following, from_left, from_right, halo, scale):
    fields, rows, tile = own.shape
    vmem = pl.BlockSpec(memory_space=pltpu.VMEM)
    state = jax.ShapeDtypeStruct((3, rows, tile), jnp.float32)
    span = tile + 4 * halo
    return pl.pallas_call(
        functools.partial(shooting_kernel, halo=halo, scale=scale),
        out_shape=(state, state, jax.ShapeDtypeStruct((rows, tile), jnp.float32)),
        in_specs=[pl.BlockSpec(memory_space=pltpu.SMEM)] + [vmem] * 5,
        out_specs=(vmem, vmem, vmem),
        scratch_shapes=[
            pltpu.VMEM((fields, span, rows), jnp.float32),
            pltpu.VMEM((3, span, rows), jnp.float32),
            pltpu.VMEM((STEPS, 2, tile, rows), jnp.float32),
        ],
        cost_estimate=pl.CostEstimate(
            flops=2 * STEPS * 60 * rows * span, transcendentals=0, bytes_accessed=4 * rows * 24 * tile
        ),
    )(trig, rotation.reshape(1, rows), own, following, from_left, from_right)


def pack_kernel(
    depths_ref, start_hbm, mask_hbm, classes_hbm, drag_hbm, cos_hbm, sin_hbm,
    own_ref, low_ref, high_ref, start_v, mask_v, classes_v, drag_v, cos_v, sin_v, sems, *, width
):
    copies = [
        pltpu.make_async_copy(source, target, sems.at[index])
        for index, (source, target) in enumerate(
            [(start_hbm, start_v), (mask_hbm, mask_v), (classes_hbm, classes_v), (drag_hbm, drag_v),
             (cos_hbm, cos_v), (sin_hbm, sin_v)]
        )
    ]
    for copy in copies:
        copy.start()
    for copy in copies:
        copy.wait()
    classes = classes_v[...]
    depth = jnp.zeros(classes.shape, jnp.float32)
    for index in range(depths_ref.shape[0]):
        depth = jnp.where(classes == index, depths_ref[index], depth)
    fields = [
        start_v[0, 0], start_v[0, 1], start_v[0, 2], mask_v[...].astype(jnp.float32), depth,
        1.0 / (1.0 + drag_v[...]), cos_v[...], sin_v[...],
    ]
    tile = own_ref.shape[-1]
    for index, field in enumerate(fields):
        own_ref[index] = field
        turned = jnp.transpose(field)
        low_ref[index * width : (index + 1) * width, :] = turned[:width]
        high_ref[index * width : (index + 1) * width, :] = turned[tile - width :]


def pack(start_states, ocean_mask, depth_class, class_depth, drag_rate, tide_cos, tide_sin, width):
    rows, tile = ocean_mask.shape
    hbm = pl.BlockSpec(memory_space=pl.ANY)
    vmem = pl.BlockSpec(memory_space=pltpu.VMEM)
    strips = jax.ShapeDtypeStruct((8 * width, rows), jnp.float32)
    return pl.pallas_call(
        functools.partial(pack_kernel, width=width),
        out_shape=(jax.ShapeDtypeStruct((8, rows, tile), jnp.float32), strips, strips),
        in_specs=[pl.BlockSpec(memory_space=pltpu.SMEM)] + [hbm] * 6,
        out_specs=(vmem, vmem, vmem),
        scratch_shapes=[
            pltpu.VMEM(start_states.shape, jnp.float32),
            pltpu.VMEM((rows, tile), jnp.int32),
            pltpu.VMEM((rows, tile), jnp.int32),
            pltpu.VMEM((rows, tile), jnp.float32),
            pltpu.VMEM((rows, tile), jnp.float32),
            pltpu.VMEM((rows, tile), jnp.float32),
            pltpu.SemaphoreType.DMA((6,)),
        ],
    )(class_depth, start_states, ocean_mask, depth_class, drag_rate, tide_cos, tide_sin)


def reduce_scatter_rows(value, axis):
    count = lax.axis_size(axis)
    pieces = value.reshape((count, value.shape[0] // count, value.shape[1]))
    return jnp.sum(lax.all_to_all(pieces, axis, 0, 0, tiled=True), axis=0)


def local(start_states, ocean_mask, depth_class, class_depth, drag_rate, tide_cos, tide_sin):
    halo = 2 * STEPS
    slice_count = lax.axis_size("tm")
    slice_index = lax.axis_index("tm")
    initial = start_states[0]
    cells = lax.axis_size("cell")
    own, low, high = pack(
        start_states, ocean_mask, depth_class, class_depth, drag_rate, tide_cos, tide_sin, 2 * halo
    )
    fields, rows, width = own.shape
    following = from_behind(initial, "tm", -1)

    def strips(at_right):
        mine = high if at_right else low
        theirs = following[..., width - halo :] if at_right else following[..., :halo]
        return jnp.concatenate([mine, lane_dense(theirs).reshape(-1, rows)], axis=0)

    from_left = lax.ppermute(strips(True), "cell", ring_pairs(cells, 1))
    from_right = lax.ppermute(strips(False), "cell", ring_pairs(cells, -1))
    phase_unit = 2.0 * math.pi / (slice_count * STEPS)
    phases = (slice_index * STEPS + jnp.arange(STEPS)).astype(jnp.float32) * phase_unit
    trig = jnp.concatenate([jnp.cos(phases), jnp.sin(phases)])
    defect, pulled, drag_grad = shooting(
        trig, coriolis(rows), own, following, from_left, from_right, halo, 1.0 / slice_count
    )
    behind = from_behind(defect, "tm", 1)
    state_grad = pulled - behind
    drag_grad = reduce_scatter_rows(drag_grad, "tm")
    return (defect[None], state_grad[None], drag_grad)


def solution(mesh):
    return jax.shard_map(
        local,
        mesh=mesh,
        in_specs=(
            P("tm", None, None, "cell"),
            P(None, "cell"),
            P(None, "cell"),
            P(),
            P(None, "cell"),
            P(None, "cell"),
            P(None, "cell"),
        ),
        out_specs=(P("tm", None, None, "cell"), P("tm", None, None, "cell"), P("tm", "cell")),
        check_vma=False,
    )
```

```python
import functools
import math

import jax
import jax.numpy as jnp
from jax import lax
from jax.experimental import pallas as pl
from jax.experimental.pallas import tpu as pltpu
from jax.sharding import PartitionSpec as P

STEPS = 8


FLUX_RATE = 0.7
PRESS_RATE = 0.7
ROTATION_RATE = 0.15


def ring_pairs(count, steps):
    return [(source, (source + steps) % count) for source in range(count)]


def lane_dense(strip):
    return jnp.swapaxes(strip, -1, -2)


def from_behind(value, axis, steps):
    return lax.ppermute(value, axis, ring_pairs(lax.axis_size(axis), steps))


def coriolis(rows_count):
    latitude = math.pi * ((jnp.arange(rows_count, dtype=jnp.float32) + 0.5) / rows_count - 0.5)
    return (ROTATION_RATE * jnp.sin(latitude))[:, None]


def shooting_kernel(
    trig_ref, rot_ref, own_ref, next_ref, left_ref, right_ref,
    defect_ref, pulled_ref, drag_ref, wide_ref, ahead_ref, stored_ref, *, halo, scale
):
    rows, tile = own_ref.shape[-2], own_ref.shape[-1]
    span = wide_ref.shape[-2]
    fields = own_ref.shape[0]
    wide = 2 * halo
    for field in range(fields):
        strip = slice(field * wide, (field + 1) * wide)
        wide_ref[field] = jnp.concatenate(
            [left_ref[strip, :], jnp.transpose(own_ref[field]), right_ref[strip, :]], axis=0
        )
    edge = jnp.zeros((halo, rows), jnp.float32)
    for field in range(next_ref.shape[0]):
        strip = slice(fields * wide + field * halo, fields * wide + (field + 1) * halo)
        ahead_ref[field] = jnp.concatenate(
            [edge, left_ref[strip, :], jnp.transpose(next_ref[field]), right_ref[strip, :], edge], axis=0
        )

    lane = lax.broadcasted_iota(jnp.int32, (span, rows), 1)
    first, last = lane == 0, lane == rows - 1
    inner = slice(wide, wide + tile)

    def cols_diff(q):
        return pltpu.roll(q, span - 1, 0) - pltpu.roll(q, 1, 0)

    def rows_diff(q):
        upper = jnp.where(last, 0.0, pltpu.roll(q, rows - 1, 1))
        lower = jnp.where(first, 0.0, pltpu.roll(q, 1, 1))
        return upper - lower

    half_flux, half_press = 0.5 * FLUX_RATE, 0.5 * PRESS_RATE
    sea, depth, retain = wide_ref[3], wide_ref[4], wide_ref[5]
    rot = rot_ref[...]
    keep = sea * retain
    height, east, north = wide_ref[0] * sea, wide_ref[1] * sea, wide_ref[2] * sea
    for step in range(STEPS):
        force = trig_ref[step] * wide_ref[6] + trig_ref[STEPS + step] * wide_ref[7]
        spread = cols_diff(depth * east) + rows_diff(depth * north)
        height = sea * (height - half_flux * spread)
        surface = height + force
        east, north = (
            keep * (east - half_press * cols_diff(surface) + rot * north),
            keep * (north - half_press * rows_diff(surface) - rot * east),
        )
        stored_ref[step, 0] = east[inner]
        stored_ref[step, 1] = north[inner]
    height = sea * (height - ahead_ref[0])
    east = sea * (east - ahead_ref[1])
    north = sea * (north - ahead_ref[2])
    defect_ref[0] = jnp.transpose(height[inner])
    defect_ref[1] = jnp.transpose(east[inner])
    defect_ref[2] = jnp.transpose(north[inner])
    half_depth_flux = 0.5 * (FLUX_RATE * depth)
    drag = jnp.zeros((tile, rows), jnp.float32)
    for back in range(STEPS):
        step = STEPS - 1 - back
        east_part = keep * east
        north_part = keep * north
        height = sea * (height + half_press * (cols_diff(east_part) + rows_diff(north_part)))
        east = east_part - rot * north_part + half_depth_flux * cols_diff(height)
        north = north_part + rot * east_part + half_depth_flux * rows_diff(height)
        drag = drag - (east_part[inner] * stored_ref[step, 0] + north_part[inner] * stored_ref[step, 1])
    sea_tile = sea[inner]
    pulled_ref[0] = jnp.transpose(sea_tile * height[inner])
    pulled_ref[1] = jnp.transpose(sea_tile * east[inner])
    pulled_ref[2] = jnp.transpose(sea_tile * north[inner])
    drag_ref[...] = jnp.transpose(drag * scale)


def shooting(trig, rotation, own, following, from_left, from_right, halo, scale):
    fields, rows, tile = own.shape
    vmem = pl.BlockSpec(memory_space=pltpu.VMEM)
    state = jax.ShapeDtypeStruct((3, rows, tile), jnp.float32)
    span = tile + 4 * halo
    return pl.pallas_call(
        functools.partial(shooting_kernel, halo=halo, scale=scale),
        out_shape=(state, state, jax.ShapeDtypeStruct((rows, tile), jnp.float32)),
        in_specs=[pl.BlockSpec(memory_space=pltpu.SMEM)] + [vmem] * 5,
        out_specs=(vmem, vmem, vmem),
        scratch_shapes=[
            pltpu.VMEM((fields, span, rows), jnp.float32),
            pltpu.VMEM((3, span, rows), jnp.float32),
            pltpu.VMEM((STEPS, 2, tile, rows), jnp.float32),
        ],
        cost_estimate=pl.CostEstimate(
            flops=2 * STEPS * 60 * rows * span, transcendentals=0, bytes_accessed=4 * rows * 24 * tile
        ),
    )(trig, rotation.reshape(1, rows), own, following, from_left, from_right)


def reduce_scatter_rows(value, axis):
    count = lax.axis_size(axis)
    pieces = value.reshape((count, value.shape[0] // count, value.shape[1]))
    return jnp.sum(lax.all_to_all(pieces, axis, 0, 0, tiled=True), axis=0)


def local(start_states, ocean_mask, depth_class, class_depth, drag_rate, tide_cos, tide_sin):
    halo = 2 * STEPS
    slice_count = lax.axis_size("tm")
    slice_index = lax.axis_index("tm")
    sea_mask = ocean_mask.astype(jnp.float32)
    classes = jnp.arange(class_depth.shape[0], dtype=jnp.int32)
    depth_field = jnp.sum(
        jnp.where(depth_class[None] == classes[:, None, None], class_depth[:, None, None], 0.0),
        axis=0,
    )
    retain = 1.0 / (1.0 + drag_rate)
    initial = start_states[0]
    cells = lax.axis_size("cell")
    own = jnp.concatenate(
        [initial, jnp.stack([sea_mask, depth_field, retain, tide_cos, tide_sin])], axis=0
    )
    fields, rows, width = own.shape
    following = from_behind(initial, "tm", -1)

    def strips(at_right):
        mine = own[..., width - 2 * halo :] if at_right else own[..., : 2 * halo]
        theirs = following[..., width - halo :] if at_right else following[..., :halo]
        return jnp.concatenate(
            [lane_dense(mine).reshape(-1, rows), lane_dense(theirs).reshape(-1, rows)], axis=0
        )

    from_left = lax.ppermute(strips(True), "cell", ring_pairs(cells, 1))
    from_right = lax.ppermute(strips(False), "cell", ring_pairs(cells, -1))
    phase_unit = 2.0 * math.pi / (slice_count * STEPS)
    phases = (slice_index * STEPS + jnp.arange(STEPS)).astype(jnp.float32) * phase_unit
    trig = jnp.concatenate([jnp.cos(phases), jnp.sin(phases)])
    defect, pulled, drag_grad = shooting(
        trig, coriolis(rows), own, following, from_left, from_right, halo, 1.0
    )
    behind = from_behind(defect, "tm", 1)
    state_grad = pulled - behind
    drag_grad = reduce_scatter_rows(drag_grad, "tm") / slice_count
    return (defect[None], state_grad[None], drag_grad)


def solution(mesh):
    return jax.shard_map(
        local,
        mesh=mesh,
        in_specs=(
            P("tm", None, None, "cell"),
            P(None, "cell"),
            P(None, "cell"),
            P(),
            P(None, "cell"),
            P(None, "cell"),
            P(None, "cell"),
        ),
        out_specs=(P("tm", None, None, "cell"), P("tm", None, None, "cell"), P("tm", "cell")),
        check_vma=False,
    )
```

```python
import functools
import math

import jax
import jax.numpy as jnp
from jax import lax
from jax.experimental import pallas as pl
from jax.experimental.pallas import tpu as pltpu
from jax.sharding import PartitionSpec as P

STEPS = 8


FLUX_RATE = 0.7
PRESS_RATE = 0.7
ROTATION_RATE = 0.15


def ring_pairs(count, steps):
    return [(source, (source + steps) % count) for source in range(count)]


def lane_dense(strip):
    return jnp.swapaxes(strip, -1, -2)


def from_behind(value, axis, steps):
    return lax.ppermute(value, axis, ring_pairs(lax.axis_size(axis), steps))


def coriolis(rows_count):
    latitude = math.pi * ((jnp.arange(rows_count, dtype=jnp.float32) + 0.5) / rows_count - 0.5)
    return (ROTATION_RATE * jnp.sin(latitude))[:, None]


def shooting_kernel(
    trig_ref, rot_ref, own_ref, next_ref, left_ref, right_ref,
    defect_ref, pulled_ref, drag_ref, wide_ref, ahead_ref, stored_ref, *, halo, scale
):
    rows, tile = own_ref.shape[-2], own_ref.shape[-1]
    span = wide_ref.shape[-2]
    fields = own_ref.shape[0]
    wide = 2 * halo
    for field in range(fields):
        strip = slice(field * wide, (field + 1) * wide)
        wide_ref[field] = jnp.concatenate(
            [left_ref[strip, :], jnp.transpose(own_ref[field]), right_ref[strip, :]], axis=0
        )
    edge = jnp.zeros((halo, rows), jnp.float32)
    for field in range(next_ref.shape[0]):
        strip = slice(fields * wide + field * halo, fields * wide + (field + 1) * halo)
        ahead_ref[field] = jnp.concatenate(
            [edge, left_ref[strip, :], jnp.transpose(next_ref[field]), right_ref[strip, :], edge], axis=0
        )

    masks = {}

    def cols_diff(q):
        count = q.shape[0]
        return pltpu.roll(q, count - 1, 0) - pltpu.roll(q, 1, 0)

    def rows_diff(q):
        count = q.shape[0]
        if count not in masks:
            lane = lax.broadcasted_iota(jnp.int32, (count, rows), 1)
            masks[count] = (lane == 0, lane == rows - 1)
        first, last = masks[count]
        upper = jnp.where(last, 0.0, pltpu.roll(q, rows - 1, 1))
        lower = jnp.where(first, 0.0, pltpu.roll(q, 1, 1))
        return upper - lower

    def statics_at(low, high):
        return [wide_ref[index, low:high, :] for index in range(3, 8)]

    def cropped(values, cut):
        return [value[cut : value.shape[0] - cut] for value in values]

    cut = 2 * (STEPS // 2)
    half_flux, half_press = 0.5 * FLUX_RATE, 0.5 * PRESS_RATE
    rot = rot_ref[...]
    low, high = 0, span
    sea, depth, retain, cosine, sine = statics_at(low, high)
    keep = sea * retain
    height, east, north = wide_ref[0] * sea, wide_ref[1] * sea, wide_ref[2] * sea
    for step in range(STEPS):
        if step == STEPS // 2:
            height, east, north = cropped((height, east, north), cut)
            low, high = low + cut, high - cut
            sea, depth, retain, cosine, sine = statics_at(low, high)
            keep = sea * retain
        force = trig_ref[step] * cosine + trig_ref[STEPS + step] * sine
        spread = cols_diff(depth * east) + rows_diff(depth * north)
        height = sea * (height - half_flux * spread)
        surface = height + force
        east, north = (
            keep * (east - half_press * cols_diff(surface) + rot * north),
            keep * (north - half_press * rows_diff(surface) - rot * east),
        )
        inner = slice(wide - low, wide - low + tile)
        stored_ref[step, 0] = east[inner]
        stored_ref[step, 1] = north[inner]
    height = sea * (height - ahead_ref[0, low:high, :])
    east = sea * (east - ahead_ref[1, low:high, :])
    north = sea * (north - ahead_ref[2, low:high, :])
    defect_ref[0] = jnp.transpose(height[inner])
    defect_ref[1] = jnp.transpose(east[inner])
    defect_ref[2] = jnp.transpose(north[inner])
    height, east, north = cropped((height, east, north), halo - low)
    low, high = halo, span - halo
    drag = jnp.zeros((tile, rows), jnp.float32)
    for back in range(STEPS):
        if back % (STEPS // 2) == 0:
            if back:
                height, east, north = cropped((height, east, north), cut)
                low, high = low + cut, high - cut
            sea, depth, retain, _, _ = statics_at(low, high)
            keep = sea * retain
            half_depth_flux = 0.5 * (FLUX_RATE * depth)
            inner = slice(wide - low, wide - low + tile)
        step = STEPS - 1 - back
        east_part = keep * east
        north_part = keep * north
        height = sea * (height + half_press * (cols_diff(east_part) + rows_diff(north_part)))
        east = east_part - rot * north_part + half_depth_flux * cols_diff(height)
        north = north_part + rot * east_part + half_depth_flux * rows_diff(height)
        drag = drag - (east_part[inner] * stored_ref[step, 0] + north_part[inner] * stored_ref[step, 1])
    sea_tile = sea[inner]
    pulled_ref[0] = jnp.transpose(sea_tile * height[inner])
    pulled_ref[1] = jnp.transpose(sea_tile * east[inner])
    pulled_ref[2] = jnp.transpose(sea_tile * north[inner])
    drag_ref[...] = jnp.transpose(drag * scale)


def shooting(trig, rotation, own, following, from_left, from_right, halo, scale):
    fields, rows, tile = own.shape
    vmem = pl.BlockSpec(memory_space=pltpu.VMEM)
    state = jax.ShapeDtypeStruct((3, rows, tile), jnp.float32)
    span = tile + 4 * halo
    return pl.pallas_call(
        functools.partial(shooting_kernel, halo=halo, scale=scale),
        out_shape=(state, state, jax.ShapeDtypeStruct((rows, tile), jnp.float32)),
        in_specs=[pl.BlockSpec(memory_space=pltpu.SMEM)] + [vmem] * 5,
        out_specs=(vmem, vmem, vmem),
        scratch_shapes=[
            pltpu.VMEM((fields, span, rows), jnp.float32),
            pltpu.VMEM((3, span, rows), jnp.float32),
            pltpu.VMEM((STEPS, 2, tile, rows), jnp.float32),
        ],
        cost_estimate=pl.CostEstimate(
            flops=2 * STEPS * 60 * rows * span, transcendentals=0, bytes_accessed=4 * rows * 24 * tile
        ),
    )(trig, rotation.reshape(1, rows), own, following, from_left, from_right)


def reduce_scatter_rows(value, axis):
    count = lax.axis_size(axis)
    pieces = value.reshape((count, value.shape[0] // count, value.shape[1]))
    return jnp.sum(lax.all_to_all(pieces, axis, 0, 0, tiled=True), axis=0)


def local(start_states, ocean_mask, depth_class, class_depth, drag_rate, tide_cos, tide_sin):
    halo = 2 * STEPS
    slice_count = lax.axis_size("tm")
    slice_index = lax.axis_index("tm")
    sea_mask = ocean_mask.astype(jnp.float32)
    classes = jnp.arange(class_depth.shape[0], dtype=jnp.int32)
    depth_field = jnp.sum(
        jnp.where(depth_class[None] == classes[:, None, None], class_depth[:, None, None], 0.0),
        axis=0,
    )
    retain = 1.0 / (1.0 + drag_rate)
    initial = start_states[0]
    cells = lax.axis_size("cell")
    own = jnp.concatenate(
        [initial, jnp.stack([sea_mask, depth_field, retain, tide_cos, tide_sin])], axis=0
    )
    fields, rows, width = own.shape
    following = from_behind(initial, "tm", -1)

    def strips(at_right):
        mine = own[..., width - 2 * halo :] if at_right else own[..., : 2 * halo]
        theirs = following[..., width - halo :] if at_right else following[..., :halo]
        return jnp.concatenate(
            [lane_dense(mine).reshape(-1, rows), lane_dense(theirs).reshape(-1, rows)], axis=0
        )

    from_left = lax.ppermute(strips(True), "cell", ring_pairs(cells, 1))
    from_right = lax.ppermute(strips(False), "cell", ring_pairs(cells, -1))
    phase_unit = 2.0 * math.pi / (slice_count * STEPS)
    phases = (slice_index * STEPS + jnp.arange(STEPS)).astype(jnp.float32) * phase_unit
    trig = jnp.concatenate([jnp.cos(phases), jnp.sin(phases)])
    defect, pulled, drag_grad = shooting(
        trig, coriolis(rows), own, following, from_left, from_right, halo, 1.0
    )
    behind = from_behind(defect, "tm", 1)
    state_grad = pulled - behind
    drag_grad = reduce_scatter_rows(drag_grad, "tm") / slice_count
    return (defect[None], state_grad[None], drag_grad)


def solution(mesh):
    return jax.shard_map(
        local,
        mesh=mesh,
        in_specs=(
            P("tm", None, None, "cell"),
            P(None, "cell"),
            P(None, "cell"),
            P(),
            P(None, "cell"),
            P(None, "cell"),
            P(None, "cell"),
        ),
        out_specs=(P("tm", None, None, "cell"), P("tm", None, None, "cell"), P("tm", "cell")),
        check_vma=False,
    )
```

```python
import functools
import math

import jax
import jax.numpy as jnp
from jax import lax
from jax.experimental import pallas as pl
from jax.experimental.pallas import tpu as pltpu
from jax.sharding import PartitionSpec as P

STEPS = 8


FLUX_RATE = 0.7
PRESS_RATE = 0.7
ROTATION_RATE = 0.15


def ring_pairs(count, steps):
    return [(source, (source + steps) % count) for source in range(count)]


def lane_dense(strip):
    return jnp.swapaxes(strip, -1, -2)


def from_behind(value, axis, steps):
    return lax.ppermute(value, axis, ring_pairs(lax.axis_size(axis), steps))


def coriolis(rows_count):
    latitude = math.pi * ((jnp.arange(rows_count, dtype=jnp.float32) + 0.5) / rows_count - 0.5)
    return (ROTATION_RATE * jnp.sin(latitude))[:, None]


def shooting_kernel(
    trig_ref, rot_ref, own_ref, next_ref, left_ref, right_ref,
    defect_ref, pulled_ref, drag_ref, wide_ref, ahead_ref, stored_ref, *, halo, scale
):
    rows, tile = own_ref.shape[-2], own_ref.shape[-1]
    span = wide_ref.shape[-2]
    fields = own_ref.shape[0]
    wide = 2 * halo
    for field in range(fields):
        strip = slice(field * wide, (field + 1) * wide)
        wide_ref[field] = jnp.concatenate(
            [left_ref[strip, :], jnp.transpose(own_ref[field]), right_ref[strip, :]], axis=0
        )
    edge = jnp.zeros((halo, rows), jnp.float32)
    for field in range(next_ref.shape[0]):
        strip = slice(fields * wide + field * halo, fields * wide + (field + 1) * halo)
        ahead_ref[field] = jnp.concatenate(
            [edge, left_ref[strip, :], jnp.transpose(next_ref[field]), right_ref[strip, :], edge], axis=0
        )

    masks = {}

    def cols_diff(q):
        count = q.shape[0]
        return pltpu.roll(q, count - 1, 0) - pltpu.roll(q, 1, 0)

    def rows_diff(q):
        count = q.shape[0]
        if count not in masks:
            lane = lax.broadcasted_iota(jnp.int32, (count, rows), 1)
            masks[count] = (lane == 0, lane == rows - 1)
        first, last = masks[count]
        upper = jnp.where(last, 0.0, pltpu.roll(q, rows - 1, 1))
        lower = jnp.where(first, 0.0, pltpu.roll(q, 1, 1))
        return upper - lower

    def statics_at(low, high):
        return [wide_ref[index, low:high, :] for index in range(3, 8)]

    def cropped(values, cut):
        return [value[cut : value.shape[0] - cut] for value in values]

    cut = 2 * (STEPS // 2)
    half_flux, half_press = 0.5 * FLUX_RATE, 0.5 * PRESS_RATE
    rot = rot_ref[...]
    low, high = 0, span
    sea, depth, retain, cosine, sine = statics_at(low, high)
    keep = sea * retain
    height, east, north = wide_ref[0] * sea, wide_ref[1] * sea, wide_ref[2] * sea
    for step in range(STEPS):
        if step == STEPS // 2:
            height, east, north = cropped((height, east, north), cut)
            low, high = low + cut, high - cut
            sea, depth, retain, cosine, sine = statics_at(low, high)
            keep = sea * retain
        force = trig_ref[step] * cosine + trig_ref[STEPS + step] * sine
        spread = cols_diff(depth * east) + rows_diff(depth * north)
        height = sea * (height - half_flux * spread)
        surface = height + force
        east, north = (
            keep * (east - half_press * cols_diff(surface) + rot * north),
            keep * (north - half_press * rows_diff(surface) - rot * east),
        )
        inner = slice(wide - low, wide - low + tile)
        stored_ref[step, 0] = east[inner]
        stored_ref[step, 1] = north[inner]
    height = sea * (height - ahead_ref[0, low:high, :])
    east = sea * (east - ahead_ref[1, low:high, :])
    north = sea * (north - ahead_ref[2, low:high, :])
    defect_ref[0] = jnp.transpose(height[inner])
    defect_ref[1] = jnp.transpose(east[inner])
    defect_ref[2] = jnp.transpose(north[inner])
    height, east, north = cropped((height, east, north), halo - low)
    low, high = halo, span - halo
    drag = jnp.zeros((tile, rows), jnp.float32)
    for back in range(STEPS):
        if back % (STEPS // 2) == 0:
            if back:
                height, east, north = cropped((height, east, north), cut)
                low, high = low + cut, high - cut
            sea, depth, retain, _, _ = statics_at(low, high)
            keep = sea * retain
            half_depth_flux = 0.5 * (FLUX_RATE * depth)
            inner = slice(wide - low, wide - low + tile)
        step = STEPS - 1 - back
        east_part = keep * east
        north_part = keep * north
        height = sea * (height + half_press * (cols_diff(east_part) + rows_diff(north_part)))
        east = east_part - rot * north_part + half_depth_flux * cols_diff(height)
        north = north_part + rot * east_part + half_depth_flux * rows_diff(height)
        drag = drag - (east_part[inner] * stored_ref[step, 0] + north_part[inner] * stored_ref[step, 1])
    sea_tile = sea[inner]
    pulled_ref[0] = jnp.transpose(sea_tile * height[inner])
    pulled_ref[1] = jnp.transpose(sea_tile * east[inner])
    pulled_ref[2] = jnp.transpose(sea_tile * north[inner])
    drag_ref[...] = jnp.transpose(drag * scale)


def shooting(trig, rotation, own, following, from_left, from_right, halo, scale):
    fields, rows, tile = own.shape
    vmem = pl.BlockSpec(memory_space=pltpu.VMEM)
    state = jax.ShapeDtypeStruct((3, rows, tile), jnp.float32)
    span = tile + 4 * halo
    return pl.pallas_call(
        functools.partial(shooting_kernel, halo=halo, scale=scale),
        out_shape=(state, state, jax.ShapeDtypeStruct((rows, tile), jnp.float32)),
        in_specs=[pl.BlockSpec(memory_space=pltpu.SMEM)] + [vmem] * 5,
        out_specs=(vmem, vmem, vmem),
        scratch_shapes=[
            pltpu.VMEM((fields, span, rows), jnp.float32),
            pltpu.VMEM((3, span, rows), jnp.float32),
            pltpu.VMEM((STEPS, 2, tile, rows), jnp.float32),
        ],
        cost_estimate=pl.CostEstimate(
            flops=2 * STEPS * 60 * rows * span, transcendentals=0, bytes_accessed=4 * rows * 24 * tile
        ),
    )(trig, rotation.reshape(1, rows), own, following, from_left, from_right)


def reduce_scatter_rows(value, axis, beside):
    count = lax.axis_size(axis)
    pieces = value.reshape((count, value.shape[0] // count, value.shape[1]))
    gathered, beside = lax.optimization_barrier((lax.all_to_all(pieces, axis, 0, 0, tiled=True), beside))
    return jnp.sum(gathered, axis=0), beside


def local(start_states, ocean_mask, depth_class, class_depth, drag_rate, tide_cos, tide_sin):
    halo = 2 * STEPS
    slice_count = lax.axis_size("tm")
    slice_index = lax.axis_index("tm")
    sea_mask = ocean_mask.astype(jnp.float32)
    classes = jnp.arange(class_depth.shape[0], dtype=jnp.int32)
    depth_field = jnp.sum(
        jnp.where(depth_class[None] == classes[:, None, None], class_depth[:, None, None], 0.0),
        axis=0,
    )
    retain = 1.0 / (1.0 + drag_rate)
    initial = start_states[0]
    cells = lax.axis_size("cell")
    own = jnp.concatenate(
        [initial, jnp.stack([sea_mask, depth_field, retain, tide_cos, tide_sin])], axis=0
    )
    fields, rows, width = own.shape
    following = from_behind(initial, "tm", -1)

    def strips(at_right):
        mine = own[..., width - 2 * halo :] if at_right else own[..., : 2 * halo]
        theirs = following[..., width - halo :] if at_right else following[..., :halo]
        return jnp.concatenate(
            [lane_dense(mine).reshape(-1, rows), lane_dense(theirs).reshape(-1, rows)], axis=0
        )

    from_left = lax.ppermute(strips(True), "cell", ring_pairs(cells, 1))
    from_right = lax.ppermute(strips(False), "cell", ring_pairs(cells, -1))
    phase_unit = 2.0 * math.pi / (slice_count * STEPS)
    phases = (slice_index * STEPS + jnp.arange(STEPS)).astype(jnp.float32) * phase_unit
    trig = jnp.concatenate([jnp.cos(phases), jnp.sin(phases)])
    defect, pulled, drag_grad = shooting(
        trig, coriolis(rows), own, following, from_left, from_right, halo, 1.0
    )
    behind = from_behind(defect, "tm", 1)
    drag_grad, state_grad = reduce_scatter_rows(drag_grad, "tm", pulled - behind)
    drag_grad = drag_grad / slice_count
    return (defect[None], state_grad[None], drag_grad)


def solution(mesh):
    return jax.shard_map(
        local,
        mesh=mesh,
        in_specs=(
            P("tm", None, None, "cell"),
            P(None, "cell"),
            P(None, "cell"),
            P(),
            P(None, "cell"),
            P(None, "cell"),
            P(None, "cell"),
        ),
        out_specs=(P("tm", None, None, "cell"), P("tm", None, None, "cell"), P("tm", "cell")),
        check_vma=False,
    )
```
